512 devices in a mesh: ctx: 16 (over z_lo, y), ch: 32 (over z_hi, x, core).
Axes of the slice: x: 4, y: 4, z: 16 (z_hi: 4, z_lo: 4; z = z_hi * 4 + z_lo), core: 2. Of those that a mesh axis runs over, the one named last changes fastest.
Arguments:
- bases_in: bfloat16 [6144, 4096], P('ctx', 'ch'), may hold values from -70 to 70
- norm_gain: float32 [4096], replicated, may hold values from 0.1 to 1.9
- w_in: bfloat16 [4096, 3, 4096], P(None, None, 'ch'), may hold values from -0.09375 to 0.09375
- feat_taps: float32 [3, 3, 4096], P(None, None, 'ch'), may hold values from -3.5 to 3.5
- long_filter: bfloat16 [4096, 128], P('ch'), may hold values from -0.5 to 0.5
- skip_gain: float32 [4096], P('ch'), may hold values from -4 to 4
- w_out: bfloat16 [4096, 4096], P('ch'), may hold values from -0.1875 to 0.1875
Outputs:
- mixed: bfloat16 [6144, 4096], P('ctx', 'ch')
The draws below stay inside these ranges and needn't reach their ends.
All inputs are finite; a program needn't handle non-finite values.
Results may differ from the reference program's by a relative error of at most 0.02.
Values may be sent and summed in bfloat16 or wider, within the bound.
No kernel may reach another device: no remote copies, remote signals or barrier semaphores. Data moves between devices by JAX's collectives and lax.ppermute only.
A program may use at most 128 MiB of HBM per device.

```python
import jax
import jax.numpy as jnp
from jax import lax

D = 4096
TAPS = 128
FEAT = 3
TOKENS = 6144
N_CH = 32


def draw_bases_in(key, part):
    key_base = jax.random.fold_in(key, 11)
    key_cols = jax.random.fold_in(key, 12)
    key_rows = jax.random.fold_in(key, 13)
    base = jax.random.truncated_normal(key_base, -4.0, 4.0, (TOKENS, D), jnp.float32)
    ramp = jnp.arange(D).astype(jnp.float32) / D - 0.5
    columns = jnp.exp(jax.random.uniform(key_cols, (D,), jnp.float32, -1.15, 1.15)) * jnp.exp(ramp * jnp.log(3.0))
    rows_scale = jnp.exp(jax.random.uniform(key_rows, (TOKENS, 1), jnp.float32, -1.15, 1.15))
    return (base * columns * rows_scale).astype(jnp.bfloat16)


def with_spikes(array, key, source, target, shards_of, factor):
    def block_of(dim):
        return (jnp.arange(array.shape[dim]) // (array.shape[dim] // shards_of)).reshape((-1,) + (1,) * (array.ndim - 1 - dim))

    first = jax.random.permutation(key, shards_of)[block_of(target)]
    other_side = (block_of(target) + shards_of // 2) % shards_of
    return jnp.where((block_of(source) == first) | (block_of(source) == other_side), factor * array, array)


def block_scale(stream_key, extent, split, least, largest):
    gain, own = 1.0, jax.random.fold_in(stream_key, 6)
    for axis_at, blocks in split:
        draws = jnp.exp(jax.random.uniform(jax.random.fold_in(own, axis_at), (blocks,), jnp.float32, least / len(split), largest / len(split)))
        gain = gain * jnp.repeat(draws, extent[axis_at] // blocks).reshape([-1 if axis == axis_at else 1 for axis in range(len(extent))])
    return gain


def noise(own_key, shape, spread, reach, cuts=(), dtype=jnp.bfloat16):
    factor_of = block_scale(own_key, shape, cuts, -0.22, 0.18) if cuts else 1.0
    result = jax.random.normal(own_key, shape, jnp.float32) * spread * factor_of
    return jnp.minimum(jnp.maximum(result, -reach), reach).astype(dtype)


def heavy_noise(stream_key, dims, width, limit, cuts, heavy, dtype=jnp.bfloat16):
    values = width * jax.random.normal(stream_key, dims, jnp.float32)
    if cuts:
        values = values * block_scale(stream_key, dims, cuts, -0.22, 0.18)
    return jnp.clip(with_spikes(values, jax.random.fold_in(stream_key, 3), *heavy), -limit, limit).astype(dtype)


def setup_inputs(seed: int = 0) -> dict:
    key_of = jax.random.split(jax.random.key(seed), 8)
    return {
        "bases_in": draw_bases_in(jax.random.fold_in(key_of[7], 71), 0),
        "norm_gain": jnp.clip(1.0 + 0.18 * jax.random.normal(key_of[1], (D,), jnp.float32), 0.1, 1.9),
        "w_in": noise(key_of[2], (D, 3, D), D ** -0.5, 0.09375, ((2, 32),)),
        "feat_taps": noise(key_of[3], (3, FEAT, D), FEAT ** -0.5, 3.5, ((2, 32),), jnp.float32),
        "long_filter": noise(key_of[4], (D, TAPS), TAPS ** -0.5, 0.5, ((0, 32),)),
        "skip_gain": noise(key_of[5], (D,), 1.0, 4.0, ((0, 32),), jnp.float32),
        "w_out": heavy_noise(key_of[6], (D, D), D ** -0.5, 0.1875, ((0, 32),), (0, 1, 32, 2.75)),
    }


def reference(bases_in, norm_gain, w_in, feat_taps, long_filter, skip_gain, w_out):
    wide = bases_in.astype(jnp.float32)
    inverse = lax.rsqrt(lax.optimization_barrier(jnp.mean(wide * wide, axis=1, keepdims=True)) + 1e-05)
    normed = (wide * inverse * norm_gain).astype(jnp.bfloat16)
    projected = jnp.dot(normed, w_in.reshape(D, 3 * D), preferred_element_type=jnp.float32)
    projected = projected.astype(jnp.bfloat16).reshape(TOKENS, 3, D)
    padded = jnp.pad(projected, ((FEAT - 1, 0), (0, 0), (0, 0)))
    feats = jnp.zeros((TOKENS, 3, D), jnp.float32)
    for tap in range(FEAT):
        feats = feats + feat_taps[:, tap, :] * padded[FEAT - 1 - tap:FEAT - 1 - tap + TOKENS].astype(jnp.float32)
    product = (feats[:, 1, :] * feats[:, 2, :]).astype(jnp.bfloat16)
    widened = product.astype(jnp.float32)
    upadded = jnp.pad(widened, ((TAPS - 1, 0), (0, 0)))
    filt_rows = long_filter.astype(jnp.float32).T

    def add_tap(tap, total):
        start = (TAPS - 1 - tap).astype(jnp.int32)
        window = lax.dynamic_slice(upadded, (start, jnp.int32(0)), (TOKENS, D))
        return total + lax.dynamic_index_in_dim(filt_rows, tap, 0, keepdims=False) * window
    filtered = lax.fori_loop(jnp.int32(0), jnp.int32(TAPS), add_tap, jnp.zeros((TOKENS, D), jnp.float32))
    gated = (feats[:, 0, :] * (filtered + skip_gain * widened)).astype(jnp.bfloat16)
    width_dev = D // N_CH
    gated_groups = gated.reshape(TOKENS, N_CH, width_dev).transpose(1, 0, 2)
    weight_groups = w_out.reshape(N_CH, width_dev, D)

    def add_group(total, pair):
        partial_sum = jnp.dot(pair[0], pair[1], preferred_element_type=jnp.float32).astype(jnp.bfloat16)
        partial_sum = lax.optimization_barrier(partial_sum)
        return (total + partial_sum.astype(jnp.float32), None)
    summed, _ = lax.scan(add_group, jnp.zeros((TOKENS, D), jnp.float32), (gated_groups, weight_groups))
    return summed.astype(jnp.bfloat16)
```

```python
import jax
import jax.numpy as jnp
from jax import lax
from jax.experimental import pallas as pl
from jax.experimental.pallas import tpu as pltpu
from jax.sharding import Mesh, PartitionSpec as P

CTX_PARTS = (("z_lo", 4), ("y", 4))
CH_PARTS = (("z_hi", 4), ("x", 4), ("core", 2))
CTX = tuple(name for name, _ in CTX_PARTS)
CH = tuple(name for name, _ in CH_PARTS)
CTX_COUNT = 16
FILTER_ROWS = 64


def passed_along(value, axis, count, steps):
    initial, last = (max(0, -steps), min(count, count - steps))
    return lax.ppermute(value, axis, [(source, source + steps) for source in range(initial, last)])


def featurize(extended, feat_taps, count):
    feat_len = feat_taps.shape[1]
    chans = feat_taps.shape[2]
    shaped = extended.reshape(extended.shape[0], 3, chans)
    feats = jnp.zeros((count, 3, chans), jnp.float32)
    for tap in range(feat_len):
        feats = feats + feat_taps[:, tap, :] * shaped[
            feat_len - 1 - tap : feat_len - 1 - tap + count
        ].astype(jnp.float32)
    return feats


def filter_kernel(ext_ref, filt_ref, out_ref, shift_ref):
    taps = filt_ref.shape[0]
    rows = shift_ref.shape[1]
    count = out_ref.shape[0]
    for b in range(8):
        shift_ref[b] = ext_ref[pl.ds(8 - b, rows), :]

    def tile(index, carry):
        base = pl.multiple_of(index * FILTER_ROWS, 8)
        acc = jnp.zeros((FILTER_ROWS, out_ref.shape[1]), jnp.float32)
        for group in range(taps // 8):
            for b in range(8):
                tap = 8 * group + b
                acc = acc + filt_ref[pl.ds(tap, 1), :] * shift_ref[
                    b, pl.ds(base + taps - 8 - 8 * group, FILTER_ROWS), :
                ]
        out_ref[pl.ds(base, FILTER_ROWS), :] = acc
        return carry

    lax.fori_loop(0, count // FILTER_ROWS, tile, 0)


def causal_filter(extended, filt_rows):
    taps, chans = filt_rows.shape
    count = extended.shape[0] - taps
    rows = extended.shape[0] - 8
    return pl.pallas_call(
        filter_kernel,
        out_shape=jax.ShapeDtypeStruct((count, chans), jnp.float32),
        scratch_shapes=[pltpu.VMEM((8, rows, chans), jnp.float32)],
    )(extended, filt_rows)


def shards(bases_in, norm_gain, w_in, feat_taps, long_filter, skip_gain, w_out):
    tok, chans = bases_in.shape
    width = norm_gain.shape[0]
    taps = long_filter.shape[1]
    feat_len = feat_taps.shape[1]
    w_flat = w_in.reshape(width, 3 * chans)
    stacked = bases_in
    for name, _ in CH_PARTS:
        stacked = lax.all_gather(stacked, name, axis=0)
    whole = stacked.transpose(3, 2, 1, 0, 4).reshape(tok, width)
    wide = whole.astype(jnp.float32)
    inverse = lax.rsqrt(jnp.mean(wide * wide, axis=1, keepdims=True) + 1e-05)
    normed = (wide * inverse * norm_gain).astype(jnp.bfloat16)
    mixed_in = jnp.dot(normed, w_flat, preferred_element_type=jnp.float32)
    projected = mixed_in.astype(jnp.bfloat16)
    earlier = passed_along(projected[tok - (feat_len - 1) :], CTX, CTX_COUNT, 1)
    feats = featurize(jnp.concatenate([earlier, projected], axis=0), feat_taps, tok)
    query = feats[:, 0, :]
    product = (feats[:, 1, :] * feats[:, 2, :]).astype(jnp.bfloat16)
    before = passed_along(product[tok - (taps - 1) :], CTX, CTX_COUNT, 1)
    extended = jnp.concatenate(
        [jnp.zeros((1, chans), jnp.bfloat16), before, product], axis=0
    ).astype(jnp.float32)
    filtered = causal_filter(extended, long_filter.astype(jnp.float32).T)
    gated = (query * (filtered + skip_gain * product.astype(jnp.float32))).astype(jnp.bfloat16)
    terms = jnp.dot(gated, w_out, preferred_element_type=jnp.float32).astype(jnp.bfloat16)
    sizes = [size for _, size in CH_PARTS]
    split = terms.reshape(tok, *sizes, chans).transpose(3, 2, 1, 0, 4)
    for name, _ in CH_PARTS[::-1]:
        split = lax.psum_scatter(split, name, scatter_dimension=0)
    return split


def solution(mesh):
    shape = [size for _, size in CTX_PARTS] + [size for _, size in CH_PARTS]
    fine = Mesh(mesh.devices.reshape(shape), CTX + CH)
    in_specs = (
        P(CTX, CH),
        P(),
        P(None, None, CH),
        P(None, None, CH),
        P(CH, None),
        P(CH),
        P(CH, None),
    )
    out_specs = P(CTX, CH)
    return jax.shard_map(shards, mesh=fine, in_specs=in_specs, out_specs=out_specs, check_vma=False)
```

```python
import jax
import jax.numpy as jnp
from jax import lax
from jax.experimental import pallas as pl
from jax.experimental.pallas import tpu as pltpu
from jax.sharding import Mesh, PartitionSpec as P

CTX_PARTS = (("z_lo", 4), ("y", 4))
CH_PARTS = (("z_hi", 4), ("x", 4), ("core", 2))
CTX = tuple(name for name, _ in CTX_PARTS)
CH = tuple(name for name, _ in CH_PARTS)
CTX_COUNT = 16
FILTER_ROWS = 64


def passed_along(value, axis, count, steps):
    initial, last = (max(0, -steps), min(count, count - steps))
    return lax.ppermute(value, axis, [(source, source + steps) for source in range(initial, last)])


def gathered(block, name, count):
    index = lax.axis_index(name)
    out = jnp.zeros((count,) + block.shape, block.dtype)
    out = lax.dynamic_update_index_in_dim(out, block, index, 0)
    for shift in range(1, count):
        got = lax.ppermute(block, name, [(k, (k + shift) % count) for k in range(count)])
        out = lax.dynamic_update_index_in_dim(out, got, (index - shift) % count, 0)
    return out


def reduced(stack, name, count):
    index = lax.axis_index(name)
    total = lax.dynamic_index_in_dim(stack, index, 0, keepdims=False).astype(jnp.float32)
    for shift in range(1, count):
        part = lax.dynamic_index_in_dim(stack, (index + shift) % count, 0, keepdims=False)
        got = lax.ppermute(part, name, [(k, (k + shift) % count) for k in range(count)])
        total = total + got.astype(jnp.float32)
    return total


def featurize(extended, feat_taps, count):
    feat_len = feat_taps.shape[1]
    chans = feat_taps.shape[2]
    shaped = extended.reshape(extended.shape[0], 3, chans)
    feats = jnp.zeros((count, 3, chans), jnp.float32)
    for tap in range(feat_len):
        feats = feats + feat_taps[:, tap, :] * shaped[
            feat_len - 1 - tap : feat_len - 1 - tap + count
        ].astype(jnp.float32)
    return feats


def filter_kernel(ext_ref, filt_ref, out_ref, shift_ref):
    taps = filt_ref.shape[0]
    rows = shift_ref.shape[1]
    count = out_ref.shape[0]
    for b in range(8):
        shift_ref[b] = ext_ref[pl.ds(8 - b, rows), :]

    def tile(index, carry):
        base = pl.multiple_of(index * FILTER_ROWS, 8)
        acc = jnp.zeros((FILTER_ROWS, out_ref.shape[1]), jnp.float32)
        for group in range(taps // 8):
            for b in range(8):
                tap = 8 * group + b
                acc = acc + filt_ref[pl.ds(tap, 1), :] * shift_ref[
                    b, pl.ds(base + taps - 8 - 8 * group, FILTER_ROWS), :
                ]
        out_ref[pl.ds(base, FILTER_ROWS), :] = acc
        return carry

    lax.fori_loop(0, count // FILTER_ROWS, tile, 0)


def causal_filter(extended, filt_rows):
    taps, chans = filt_rows.shape
    count = extended.shape[0] - taps
    rows = extended.shape[0] - 8
    return pl.pallas_call(
        filter_kernel,
        out_shape=jax.ShapeDtypeStruct((count, chans), jnp.float32),
        scratch_shapes=[pltpu.VMEM((8, rows, chans), jnp.float32)],
    )(extended, filt_rows)


def shards(bases_in, norm_gain, w_in, feat_taps, long_filter, skip_gain, w_out):
    tok, chans = bases_in.shape
    width = norm_gain.shape[0]
    taps = long_filter.shape[1]
    feat_len = feat_taps.shape[1]
    w_flat = w_in.reshape(width, 3 * chans)
    stacked = bases_in
    for name, size in CH_PARTS:
        stacked = gathered(stacked, name, size)
    whole = stacked.transpose(3, 2, 1, 0, 4).reshape(tok, width)
    wide = whole.astype(jnp.float32)
    inverse = lax.rsqrt(jnp.mean(wide * wide, axis=1, keepdims=True) + 1e-05)
    normed = (wide * inverse * norm_gain).astype(jnp.bfloat16)
    mixed_in = jnp.dot(normed, w_flat, preferred_element_type=jnp.float32)
    projected = mixed_in.astype(jnp.bfloat16)
    earlier = passed_along(projected[tok - (feat_len - 1) :], CTX, CTX_COUNT, 1)
    feats = featurize(jnp.concatenate([earlier, projected], axis=0), feat_taps, tok)
    query = feats[:, 0, :]
    product = (feats[:, 1, :] * feats[:, 2, :]).astype(jnp.bfloat16)
    before = passed_along(product[tok - (taps - 1) :], CTX, CTX_COUNT, 1)
    extended = jnp.concatenate(
        [jnp.zeros((1, chans), jnp.bfloat16), before, product], axis=0
    ).astype(jnp.float32)
    filtered = causal_filter(extended, long_filter.astype(jnp.float32).T)
    gated = (query * (filtered + skip_gain * product.astype(jnp.float32))).astype(jnp.bfloat16)
    terms = jnp.dot(gated, w_out, preferred_element_type=jnp.float32).astype(jnp.bfloat16)
    sizes = [size for _, size in CH_PARTS]
    split = terms.reshape(tok, *sizes, chans).transpose(3, 2, 1, 0, 4)
    for name, size in CH_PARTS[::-1]:
        split = reduced(split, name, size).astype(jnp.bfloat16)
    return split


def solution(mesh):
    shape = [size for _, size in CTX_PARTS] + [size for _, size in CH_PARTS]
    fine = Mesh(mesh.devices.reshape(shape), CTX + CH)
    in_specs = (
        P(CTX, CH),
        P(),
        P(None, None, CH),
        P(None, None, CH),
        P(CH, None),
        P(CH),
        P(CH, None),
    )
    out_specs = P(CTX, CH)
    return jax.shard_map(shards, mesh=fine, in_specs=in_specs, out_specs=out_specs, check_vma=False)
```

```python
import jax
import jax.numpy as jnp
from jax import lax
from jax.experimental import pallas as pl
from jax.experimental.pallas import tpu as pltpu
from jax.sharding import Mesh, PartitionSpec as P

CTX_PARTS = (("z_lo", 4), ("y", 4))
CH_PARTS = (("z_hi", 4), ("x", 4), ("core", 2))
CTX = tuple(name for name, _ in CTX_PARTS)
CH = tuple(name for name, _ in CH_PARTS)
CTX_COUNT = 16
FILTER_ROWS = 64


def passed_along(value, axis, count, steps):
    initial, last = (max(0, -steps), min(count, count - steps))
    return lax.ppermute(value, axis, [(source, source + steps) for source in range(initial, last)])


def shifted(value, name, count, steps):
    return lax.ppermute(value, name, [(k, (k + steps) % count) for k in range(count)])


def halves(value):
    half = value.shape[-2] // 2
    return value[..., :half, :], value[..., half:, :]


def gathered(block, name, count):
    index = lax.axis_index(name)
    out = jnp.zeros((count,) + block.shape, block.dtype)
    out = lax.dynamic_update_index_in_dim(out, block, index, 0)
    if count == 2:
        return lax.dynamic_update_index_in_dim(out, shifted(block, name, 2, 1), 1 - index, 0)
    left = shifted(block, name, count, 1)
    right = shifted(block, name, count, -1)
    far = jnp.concatenate(
        [shifted(halves(left)[0], name, count, 1), shifted(halves(right)[1], name, count, -1)], axis=-2
    )
    out = lax.dynamic_update_index_in_dim(out, left, (index - 1) % count, 0)
    out = lax.dynamic_update_index_in_dim(out, right, (index + 1) % count, 0)
    return lax.dynamic_update_index_in_dim(out, far, (index + 2) % count, 0)


def reduced(stack, name, count):
    own = stack[0].astype(jnp.float32)
    if count == 2:
        return own + shifted(stack[1], name, 2, 1).astype(jnp.float32)
    far_a, far_b = halves(stack[2])
    from_left = shifted(far_a, name, count, 1).astype(jnp.float32)
    from_right = shifted(far_b, name, count, -1).astype(jnp.float32)
    next_a, next_b = halves(stack[1])
    prev_a, prev_b = halves(stack[3])
    to_next = jnp.concatenate([(next_a.astype(jnp.float32) + from_left).astype(jnp.bfloat16), next_b], axis=-2)
    to_prev = jnp.concatenate([prev_a, (prev_b.astype(jnp.float32) + from_right).astype(jnp.bfloat16)], axis=-2)
    total = own + shifted(to_next, name, count, 1).astype(jnp.float32)
    return total + shifted(to_prev, name, count, -1).astype(jnp.float32)


def featurize(extended, feat_taps, count):
    feat_len = feat_taps.shape[1]
    chans = feat_taps.shape[2]
    shaped = extended.reshape(extended.shape[0], 3, chans)
    feats = jnp.zeros((count, 3, chans), jnp.float32)
    for tap in range(feat_len):
        feats = feats + feat_taps[:, tap, :] * shaped[
            feat_len - 1 - tap : feat_len - 1 - tap + count
        ].astype(jnp.float32)
    return feats


def filter_kernel(ext_ref, filt_ref, out_ref, shift_ref):
    taps = filt_ref.shape[0]
    rows = shift_ref.shape[1]
    count = out_ref.shape[0]
    for b in range(8):
        shift_ref[b] = ext_ref[pl.ds(8 - b, rows), :]

    def tile(index, carry):
        base = pl.multiple_of(index * FILTER_ROWS, 8)
        acc = jnp.zeros((FILTER_ROWS, out_ref.shape[1]), jnp.float32)
        for group in range(taps // 8):
            for b in range(8):
                tap = 8 * group + b
                acc = acc + filt_ref[pl.ds(tap, 1), :] * shift_ref[
                    b, pl.ds(base + taps - 8 - 8 * group, FILTER_ROWS), :
                ]
        out_ref[pl.ds(base, FILTER_ROWS), :] = acc
        return carry

    lax.fori_loop(0, count // FILTER_ROWS, tile, 0)


def causal_filter(extended, filt_rows):
    taps, chans = filt_rows.shape
    count = extended.shape[0] - taps
    rows = extended.shape[0] - 8
    return pl.pallas_call(
        filter_kernel,
        out_shape=jax.ShapeDtypeStruct((count, chans), jnp.float32),
        scratch_shapes=[pltpu.VMEM((8, rows, chans), jnp.float32)],
    )(extended, filt_rows)


def shards(bases_in, norm_gain, w_in, feat_taps, long_filter, skip_gain, w_out):
    tok, chans = bases_in.shape
    width = norm_gain.shape[0]
    taps = long_filter.shape[1]
    feat_len = feat_taps.shape[1]
    w_flat = w_in.reshape(width, 3 * chans)
    stacked = bases_in
    for name, size in CH_PARTS:
        stacked = gathered(stacked, name, size)
    whole = stacked.transpose(3, 2, 1, 0, 4).reshape(tok, width)
    wide = whole.astype(jnp.float32)
    inverse = lax.rsqrt(jnp.mean(wide * wide, axis=1, keepdims=True) + 1e-05)
    normed = (wide * inverse * norm_gain).astype(jnp.bfloat16)
    mixed_in = jnp.dot(normed, w_flat, preferred_element_type=jnp.float32)
    projected = mixed_in.astype(jnp.bfloat16)
    earlier = passed_along(projected[tok - (feat_len - 1) :], CTX, CTX_COUNT, 1)
    feats = featurize(jnp.concatenate([earlier, projected], axis=0), feat_taps, tok)
    query = feats[:, 0, :]
    product = (feats[:, 1, :] * feats[:, 2, :]).astype(jnp.bfloat16)
    before = passed_along(product[tok - (taps - 1) :], CTX, CTX_COUNT, 1)
    extended = jnp.concatenate(
        [jnp.zeros((1, chans), jnp.bfloat16), before, product], axis=0
    ).astype(jnp.float32)
    filtered = causal_filter(extended, long_filter.astype(jnp.float32).T)
    gated = (query * (filtered + skip_gain * product.astype(jnp.float32))).astype(jnp.bfloat16)
    sizes = [size for _, size in CH_PARTS]
    blocks = w_out.reshape(chans, *sizes, chans)
    for axis, (name, _) in enumerate(CH_PARTS):
        blocks = jnp.roll(blocks, -lax.axis_index(name), axis=axis + 1)
    blocks = blocks.transpose(3, 2, 1, 0, 4)
    split = jnp.einsum(
        "tk,cxzki->cxzti", gated, blocks, preferred_element_type=jnp.float32
    ).astype(jnp.bfloat16)
    for name, size in CH_PARTS[::-1]:
        split = reduced(split, name, size).astype(jnp.bfloat16)
    return split


def solution(mesh):
    shape = [size for _, size in CTX_PARTS] + [size for _, size in CH_PARTS]
    fine = Mesh(mesh.devices.reshape(shape), CTX + CH)
    in_specs = (
        P(CTX, CH),
        P(),
        P(None, None, CH),
        P(None, None, CH),
        P(CH, None),
        P(CH),
        P(CH, None),
    )
    out_specs = P(CTX, CH)
    return jax.shard_map(shards, mesh=fine, in_specs=in_specs, out_specs=out_specs, check_vma=False)
```

```python
import jax
import jax.numpy as jnp
from jax import lax
from jax.experimental import pallas as pl
from jax.experimental.pallas import tpu as pltpu
from jax.sharding import Mesh, PartitionSpec as P

CTX_PARTS = (("z_lo", 4), ("y", 4))
CH_PARTS = (("z_hi", 4), ("x", 4), ("core", 2))
CTX = tuple(name for name, _ in CTX_PARTS)
CH = tuple(name for name, _ in CH_PARTS)
CTX_COUNT = 16
FILTER_ROWS = 64


def passed_along(value, axis, count, steps):
    initial, last = (max(0, -steps), min(count, count - steps))
    return lax.ppermute(value, axis, [(source, source + steps) for source in range(initial, last)])


def gathered(block, name, count):
    copies = jnp.broadcast_to(block[None], (count,) + block.shape)
    return lax.all_to_all(copies, name, 0, 0)


def reduced(stack, name, count):
    parts = lax.all_to_all(stack, name, 0, 0)
    total = parts[0].astype(jnp.float32)
    for member in range(1, count):
        total = total + parts[member].astype(jnp.float32)
    return total


def featurize(extended, feat_taps, count):
    feat_len = feat_taps.shape[1]
    chans = feat_taps.shape[2]
    shaped = extended.reshape(extended.shape[0], 3, chans)
    feats = jnp.zeros((count, 3, chans), jnp.float32)
    for tap in range(feat_len):
        feats = feats + feat_taps[:, tap, :] * shaped[
            feat_len - 1 - tap : feat_len - 1 - tap + count
        ].astype(jnp.float32)
    return feats


def filter_kernel(ext_ref, filt_ref, out_ref, shift_ref):
    taps = filt_ref.shape[0]
    rows = shift_ref.shape[1]
    count = out_ref.shape[0]
    for b in range(8):
        shift_ref[b] = ext_ref[pl.ds(8 - b, rows), :]

    def tile(index, carry):
        base = pl.multiple_of(index * FILTER_ROWS, 8)
        acc = jnp.zeros((FILTER_ROWS, out_ref.shape[1]), jnp.float32)
        for group in range(taps // 8):
            for b in range(8):
                tap = 8 * group + b
                acc = acc + filt_ref[pl.ds(tap, 1), :] * shift_ref[
                    b, pl.ds(base + taps - 8 - 8 * group, FILTER_ROWS), :
                ]
        out_ref[pl.ds(base, FILTER_ROWS), :] = acc
        return carry

    lax.fori_loop(0, count // FILTER_ROWS, tile, 0)


def causal_filter(extended, filt_rows):
    taps, chans = filt_rows.shape
    count = extended.shape[0] - taps
    rows = extended.shape[0] - 8
    return pl.pallas_call(
        filter_kernel,
        out_shape=jax.ShapeDtypeStruct((count, chans), jnp.float32),
        scratch_shapes=[pltpu.VMEM((8, rows, chans), jnp.float32)],
    )(extended, filt_rows)


def shards(bases_in, norm_gain, w_in, feat_taps, long_filter, skip_gain, w_out):
    tok, chans = bases_in.shape
    width = norm_gain.shape[0]
    taps = long_filter.shape[1]
    feat_len = feat_taps.shape[1]
    w_flat = w_in.reshape(width, 3 * chans)
    stacked = bases_in
    for name, size in CH_PARTS:
        stacked = gathered(stacked, name, size)
    whole = stacked.transpose(3, 2, 1, 0, 4).reshape(tok, width)
    wide = whole.astype(jnp.float32)
    inverse = lax.rsqrt(jnp.mean(wide * wide, axis=1, keepdims=True) + 1e-05)
    normed = (wide * inverse * norm_gain).astype(jnp.bfloat16)
    mixed_in = jnp.dot(normed, w_flat, preferred_element_type=jnp.float32)
    projected = mixed_in.astype(jnp.bfloat16)
    earlier = passed_along(projected[tok - (feat_len - 1) :], CTX, CTX_COUNT, 1)
    feats = featurize(jnp.concatenate([earlier, projected], axis=0), feat_taps, tok)
    query = feats[:, 0, :]
    product = (feats[:, 1, :] * feats[:, 2, :]).astype(jnp.bfloat16)
    before = passed_along(product[tok - (taps - 1) :], CTX, CTX_COUNT, 1)
    extended = jnp.concatenate(
        [jnp.zeros((1, chans), jnp.bfloat16), before, product], axis=0
    ).astype(jnp.float32)
    filtered = causal_filter(extended, long_filter.astype(jnp.float32).T)
    gated = (query * (filtered + skip_gain * product.astype(jnp.float32))).astype(jnp.bfloat16)
    sizes = [size for _, size in CH_PARTS]
    blocks = w_out.reshape(chans, *sizes, chans).transpose(3, 2, 1, 0, 4)
    split = jnp.einsum(
        "tk,cxzki->cxzti", gated, blocks, preferred_element_type=jnp.float32
    ).astype(jnp.bfloat16)
    for name, size in CH_PARTS[::-1]:
        split = reduced(split, name, size).astype(jnp.bfloat16)
    return split


def solution(mesh):
    shape = [size for _, size in CTX_PARTS] + [size for _, size in CH_PARTS]
    fine = Mesh(mesh.devices.reshape(shape), CTX + CH)
    in_specs = (
        P(CTX, CH),
        P(),
        P(None, None, CH),
        P(None, None, CH),
        P(CH, None),
        P(CH),
        P(CH, None),
    )
    out_specs = P(CTX, CH)
    return jax.shard_map(shards, mesh=fine, in_specs=in_specs, out_specs=out_specs, check_vma=False)
```

```python
import jax
import jax.numpy as jnp
from jax import lax
from jax.experimental import pallas as pl
from jax.experimental.pallas import tpu as pltpu
from jax.sharding import Mesh, PartitionSpec as P

CTX_PARTS = (("z_lo", 4), ("y", 4))
CH_PARTS = (("z_hi", 4), ("x", 4), ("core", 2))
CTX = tuple(name for name, _ in CTX_PARTS)
CH = tuple(name for name, _ in CH_PARTS)
CTX_COUNT = 16
FILTER_ROWS = 64


def passed_along(value, axis, count, steps):
    initial, last = (max(0, -steps), min(count, count - steps))
    return lax.ppermute(value, axis, [(source, source + steps) for source in range(initial, last)])


def gathered(block, name, count):
    copies = jnp.broadcast_to(block[None], (count,) + block.shape)
    return lax.all_to_all(copies, name, 0, 0)


def reduced(stack, name, count):
    parts = lax.all_to_all(stack, name, 0, 0)
    total = parts[0].astype(jnp.float32)
    for member in range(1, count):
        total = total + parts[member].astype(jnp.float32)
    return total


def featurize(extended, feat_taps, count):
    feat_len = feat_taps.shape[1]
    chans = feat_taps.shape[2]
    shaped = extended.reshape(extended.shape[0], 3, chans)
    feats = jnp.zeros((count, 3, chans), jnp.float32)
    for tap in range(feat_len):
        feats = feats + feat_taps[:, tap, :] * shaped[
            feat_len - 1 - tap : feat_len - 1 - tap + count
        ].astype(jnp.float32)
    return feats


def filter_kernel(ext_ref, filt_ref, out_ref, shift_ref):
    taps = filt_ref.shape[0]
    rows = shift_ref.shape[1]
    count = out_ref.shape[0]
    for b in range(8):
        shift_ref[b] = ext_ref[pl.ds(8 - b, rows), :]

    def tile(index, carry):
        base = pl.multiple_of(index * FILTER_ROWS, 8)
        acc = jnp.zeros((FILTER_ROWS, out_ref.shape[1]), jnp.float32)
        for group in range(taps // 8):
            for b in range(8):
                tap = 8 * group + b
                acc = acc + filt_ref[pl.ds(tap, 1), :] * shift_ref[
                    b, pl.ds(base + taps - 8 - 8 * group, FILTER_ROWS), :
                ]
        out_ref[pl.ds(base, FILTER_ROWS), :] = acc
        return carry

    lax.fori_loop(0, count // FILTER_ROWS, tile, 0)


def causal_filter(extended, filt_rows):
    taps, chans = filt_rows.shape
    count = extended.shape[0] - taps
    rows = extended.shape[0] - 8
    return pl.pallas_call(
        filter_kernel,
        out_shape=jax.ShapeDtypeStruct((count, chans), jnp.float32),
        scratch_shapes=[pltpu.VMEM((8, rows, chans), jnp.float32)],
    )(extended, filt_rows)


def shards(bases_in, norm_gain, w_in, feat_taps, long_filter, skip_gain, w_out):
    tok, chans = bases_in.shape
    width = norm_gain.shape[0]
    taps = long_filter.shape[1]
    feat_len = feat_taps.shape[1]
    w_flat = w_in.reshape(width, 3 * chans)
    stacked = bases_in
    for name, size in CH_PARTS:
        stacked = gathered(stacked, name, size)
    whole = stacked.transpose(3, 2, 1, 0, 4).reshape(tok, width)
    wide = whole.astype(jnp.float32)
    inverse = lax.rsqrt(jnp.mean(wide * wide, axis=1, keepdims=True) + 1e-05)
    normed = (wide * inverse * norm_gain).astype(jnp.bfloat16)
    mixed_in = jnp.dot(normed, w_flat, preferred_element_type=jnp.float32)
    projected = mixed_in.astype(jnp.bfloat16)
    earlier = passed_along(projected[tok - (taps - 1) - (feat_len - 1) :], CTX, CTX_COUNT, 1)
    early_feats = featurize(earlier, feat_taps, taps - 1)
    before = (early_feats[:, 1, :] * early_feats[:, 2, :]).astype(jnp.bfloat16)
    feats = featurize(
        jnp.concatenate([earlier[earlier.shape[0] - (feat_len - 1) :], projected], axis=0), feat_taps, tok
    )
    query = feats[:, 0, :]
    product = (feats[:, 1, :] * feats[:, 2, :]).astype(jnp.bfloat16)
    extended = jnp.concatenate(
        [jnp.zeros((1, chans), jnp.bfloat16), before, product], axis=0
    ).astype(jnp.float32)
    filtered = causal_filter(extended, long_filter.astype(jnp.float32).T)
    gated = (query * (filtered + skip_gain * product.astype(jnp.float32))).astype(jnp.bfloat16)
    sizes = [size for _, size in CH_PARTS]
    blocks = w_out.reshape(chans, *sizes, chans).transpose(3, 2, 1, 0, 4)
    split = jnp.einsum(
        "tk,cxzki->cxzti", gated, blocks, preferred_element_type=jnp.float32
    ).astype(jnp.bfloat16)
    for name, size in CH_PARTS[::-1]:
        split = reduced(split, name, size).astype(jnp.bfloat16)
    return split


def solution(mesh):
    shape = [size for _, size in CTX_PARTS] + [size for _, size in CH_PARTS]
    fine = Mesh(mesh.devices.reshape(shape), CTX + CH)
    in_specs = (
        P(CTX, CH),
        P(),
        P(None, None, CH),
        P(None, None, CH),
        P(CH, None),
        P(CH),
        P(CH, None),
    )
    out_specs = P(CTX, CH)
    return jax.shard_map(shards, mesh=fine, in_specs=in_specs, out_specs=out_specs, check_vma=False)
```

```python
import jax
import jax.numpy as jnp
from jax import lax
from jax.experimental import pallas as pl
from jax.experimental.pallas import tpu as pltpu
from jax.sharding import Mesh, PartitionSpec as P

CTX_PARTS = (("z_lo", 4), ("y", 4))
CH_PARTS = (("z_hi", 4), ("x", 4), ("core", 2))
CTX = tuple(name for name, _ in CTX_PARTS)
CH = tuple(name for name, _ in CH_PARTS)
CTX_COUNT = 16
FILTER_ROWS = 64


def passed_along(value, axis, count, steps):
    initial, last = (max(0, -steps), min(count, count - steps))
    return lax.ppermute(value, axis, [(source, source + steps) for source in range(initial, last)])


def shifted(value, name, count, steps):
    return lax.ppermute(value, name, [(k, (k + steps) % count) for k in range(count)])


def halves(value):
    half = value.shape[-2] // 2
    return value[..., :half, :], value[..., half:, :]


def gathered(block, name, count):
    index = lax.axis_index(name)
    out = jnp.zeros((count,) + block.shape, block.dtype)
    out = lax.dynamic_update_index_in_dim(out, block, index, 0)
    if count == 2:
        return lax.dynamic_update_index_in_dim(out, shifted(block, name, 2, 1), 1 - index, 0)
    left = shifted(block, name, count, 1)
    right = shifted(block, name, count, -1)
    far = jnp.concatenate(
        [shifted(halves(block)[0], name, count, 2), shifted(halves(right)[1], name, count, -1)], axis=-2
    )
    out = lax.dynamic_update_index_in_dim(out, left, (index - 1) % count, 0)
    out = lax.dynamic_update_index_in_dim(out, right, (index + 1) % count, 0)
    return lax.dynamic_update_index_in_dim(out, far, (index + 2) % count, 0)


def reduced(stack, name, count):
    own = stack[0].astype(jnp.float32)
    if count == 2:
        return own + shifted(stack[1], name, 2, 1).astype(jnp.float32)
    far_a, far_b = halves(stack[2])
    straight = shifted(far_a, name, count, 2).astype(jnp.float32)
    passed = shifted(far_b, name, count, -1).astype(jnp.float32)
    from_left = shifted(stack[1], name, count, 1).astype(jnp.float32)
    prev_a, prev_b = halves(stack[3])
    to_prev = jnp.concatenate([prev_a, (prev_b.astype(jnp.float32) + passed).astype(jnp.bfloat16)], axis=-2)
    total = own + from_left + shifted(to_prev, name, count, -1).astype(jnp.float32)
    total_a, total_b = halves(total)
    return jnp.concatenate([total_a + straight, total_b], axis=-2)


def featurize(extended, feat_taps, count):
    feat_len = feat_taps.shape[1]
    chans = feat_taps.shape[2]
    shaped = extended.reshape(extended.shape[0], 3, chans)
    feats = jnp.zeros((count, 3, chans), jnp.float32)
    for tap in range(feat_len):
        feats = feats + feat_taps[:, tap, :] * shaped[
            feat_len - 1 - tap : feat_len - 1 - tap + count
        ].astype(jnp.float32)
    return feats


def filter_kernel(ext_ref, filt_ref, out_ref, shift_ref):
    taps = filt_ref.shape[0]
    rows = shift_ref.shape[1]
    count = out_ref.shape[0]
    for b in range(8):
        shift_ref[b] = ext_ref[pl.ds(8 - b, rows), :]

    def tile(index, carry):
        base = pl.multiple_of(index * FILTER_ROWS, 8)
        acc = jnp.zeros((FILTER_ROWS, out_ref.shape[1]), jnp.float32)
        for group in range(taps // 8):
            for b in range(8):
                tap = 8 * group + b
                acc = acc + filt_ref[pl.ds(tap, 1), :] * shift_ref[
                    b, pl.ds(base + taps - 8 - 8 * group, FILTER_ROWS), :
                ]
        out_ref[pl.ds(base, FILTER_ROWS), :] = acc
        return carry

    lax.fori_loop(0, count // FILTER_ROWS, tile, 0)


def causal_filter(extended, filt_rows):
    taps, chans = filt_rows.shape
    count = extended.shape[0] - taps
    rows = extended.shape[0] - 8
    return pl.pallas_call(
        filter_kernel,
        out_shape=jax.ShapeDtypeStruct((count, chans), jnp.float32),
        scratch_shapes=[pltpu.VMEM((8, rows, chans), jnp.float32)],
    )(extended, filt_rows)


def shards(bases_in, norm_gain, w_in, feat_taps, long_filter, skip_gain, w_out):
    tok, chans = bases_in.shape
    width = norm_gain.shape[0]
    taps = long_filter.shape[1]
    feat_len = feat_taps.shape[1]
    w_flat = w_in.reshape(width, 3 * chans)
    stacked = bases_in
    for name, size in CH_PARTS:
        stacked = gathered(stacked, name, size)
    whole = stacked.transpose(3, 2, 1, 0, 4).reshape(tok, width)
    wide = whole.astype(jnp.float32)
    inverse = lax.rsqrt(jnp.mean(wide * wide, axis=1, keepdims=True) + 1e-05)
    normed = (wide * inverse * norm_gain).astype(jnp.bfloat16)
    mixed_in = jnp.dot(normed, w_flat, preferred_element_type=jnp.float32)
    projected = mixed_in.astype(jnp.bfloat16)
    earlier = passed_along(projected[tok - (taps - 1) - (feat_len - 1) :], CTX, CTX_COUNT, 1)
    early_feats = featurize(earlier, feat_taps, taps - 1)
    before = (early_feats[:, 1, :] * early_feats[:, 2, :]).astype(jnp.bfloat16)
    feats = featurize(
        jnp.concatenate([earlier[earlier.shape[0] - (feat_len - 1) :], projected], axis=0), feat_taps, tok
    )
    query = feats[:, 0, :]
    product = (feats[:, 1, :] * feats[:, 2, :]).astype(jnp.bfloat16)
    extended = jnp.concatenate(
        [jnp.zeros((1, chans), jnp.bfloat16), before, product], axis=0
    ).astype(jnp.float32)
    filtered = causal_filter(extended, long_filter.astype(jnp.float32).T)
    gated = (query * (filtered + skip_gain * product.astype(jnp.float32))).astype(jnp.bfloat16)
    sizes = [size for _, size in CH_PARTS]
    blocks = w_out.reshape(chans, *sizes, chans)
    for axis, (name, _) in enumerate(CH_PARTS):
        blocks = jnp.roll(blocks, -lax.axis_index(name), axis=axis + 1)
    blocks = blocks.transpose(3, 2, 1, 0, 4)
    split = jnp.einsum(
        "tk,cxzki->cxzti", gated, blocks, preferred_element_type=jnp.float32
    ).astype(jnp.bfloat16)
    for name, size in CH_PARTS[::-1]:
        split = reduced(split, name, size).astype(jnp.bfloat16)
    return split


def solution(mesh):
    shape = [size for _, size in CTX_PARTS] + [size for _, size in CH_PARTS]
    fine = Mesh(mesh.devices.reshape(shape), CTX + CH)
    in_specs = (
        P(CTX, CH),
        P(),
        P(None, None, CH),
        P(None, None, CH),
        P(CH, None),
        P(CH),
        P(CH, None),
    )
    out_specs = P(CTX, CH)
    return jax.shard_map(shards, mesh=fine, in_specs=in_specs, out_specs=out_specs, check_vma=False)
```

```python
import jax
import jax.numpy as jnp
from jax import lax
from jax.experimental import pallas as pl
from jax.experimental.pallas import tpu as pltpu
from jax.sharding import Mesh, PartitionSpec as P

CTX_PARTS = (("z_lo", 4), ("y", 4))
CH_PARTS = (("z_hi", 4), ("x", 4), ("core", 2))
CTX = tuple(name for name, _ in CTX_PARTS)
CH = tuple(name for name, _ in CH_PARTS)
CTX_COUNT = 16
FILTER_ROWS = 64


def passed_along(value, axis, count, steps):
    initial, last = (max(0, -steps), min(count, count - steps))
    return lax.ppermute(value, axis, [(source, source + steps) for source in range(initial, last)])


def gathered(block, name, count):
    copies = jnp.broadcast_to(block[None], (count,) + block.shape)
    return lax.all_to_all(copies, name, 0, 0)


def reduced(stack, name, count):
    parts = lax.all_to_all(stack, name, 0, 0)
    total = parts[0].astype(jnp.float32)
    for member in range(1, count):
        total = total + parts[member].astype(jnp.float32)
    return total


def featurize(extended, feat_taps, count):
    feat_len = feat_taps.shape[1]
    chans = feat_taps.shape[2]
    shaped = extended.reshape(extended.shape[0], 3, chans)
    feats = jnp.zeros((count, 3, chans), jnp.float32)
    for tap in range(feat_len):
        feats = feats + feat_taps[:, tap, :] * shaped[
            feat_len - 1 - tap : feat_len - 1 - tap + count
        ].astype(jnp.float32)
    return feats


def filter_kernel(ext_ref, filt_ref, out_ref, shift_ref):
    taps = filt_ref.shape[0]
    rows = shift_ref.shape[1]
    count = out_ref.shape[0]
    for b in range(8):
        shift_ref[b] = ext_ref[pl.ds(8 - b, rows), :]

    def tile(index, carry):
        base = pl.multiple_of(index * FILTER_ROWS, 8)
        acc = jnp.zeros((FILTER_ROWS, out_ref.shape[1]), jnp.float32)
        for group in range(taps // 8):
            for b in range(8):
                tap = 8 * group + b
                acc = acc + filt_ref[pl.ds(tap, 1), :] * shift_ref[
                    b, pl.ds(base + taps - 8 - 8 * group, FILTER_ROWS), :
                ]
        out_ref[pl.ds(base, FILTER_ROWS), :] = acc
        return carry

    lax.fori_loop(0, count // FILTER_ROWS, tile, 0)


def causal_filter(extended, filt_rows):
    taps, chans = filt_rows.shape
    count = extended.shape[0] - taps
    rows = extended.shape[0] - 8
    return pl.pallas_call(
        filter_kernel,
        out_shape=jax.ShapeDtypeStruct((count, chans), jnp.float32),
        scratch_shapes=[pltpu.VMEM((8, rows, chans), jnp.float32)],
    )(extended, filt_rows)


def shards(bases_in, norm_gain, w_in, feat_taps, long_filter, skip_gain, w_out):
    tok, chans = bases_in.shape
    width = norm_gain.shape[0]
    taps = long_filter.shape[1]
    feat_len = feat_taps.shape[1]
    w_flat = w_in.reshape(width, 3 * chans)
    stacked = lax.all_gather(bases_in, CH[0], axis=0)
    half = tok // 2
    stacked = jnp.concatenate(
        [lax.all_gather(part, CH[1], axis=0) for part in (stacked[:, :half], stacked[:, half:])], axis=-2
    )
    stacked = gathered(stacked, CH[2], CH_PARTS[2][1])
    whole = stacked.transpose(3, 2, 1, 0, 4).reshape(tok, width)
    wide = whole.astype(jnp.float32)
    inverse = lax.rsqrt(jnp.mean(wide * wide, axis=1, keepdims=True) + 1e-05)
    normed = (wide * inverse * norm_gain).astype(jnp.bfloat16)
    mixed_in = jnp.dot(normed, w_flat, preferred_element_type=jnp.float32)
    projected = mixed_in.astype(jnp.bfloat16)
    earlier = passed_along(projected[tok - (taps - 1) - (feat_len - 1) :], CTX, CTX_COUNT, 1)
    early_feats = featurize(earlier, feat_taps, taps - 1)
    before = (early_feats[:, 1, :] * early_feats[:, 2, :]).astype(jnp.bfloat16)
    feats = featurize(
        jnp.concatenate([earlier[earlier.shape[0] - (feat_len - 1) :], projected], axis=0), feat_taps, tok
    )
    query = feats[:, 0, :]
    product = (feats[:, 1, :] * feats[:, 2, :]).astype(jnp.bfloat16)
    extended = jnp.concatenate(
        [jnp.zeros((1, chans), jnp.bfloat16), before, product], axis=0
    ).astype(jnp.float32)
    filtered = causal_filter(extended, long_filter.astype(jnp.float32).T)
    gated = (query * (filtered + skip_gain * product.astype(jnp.float32))).astype(jnp.bfloat16)
    sizes = [size for _, size in CH_PARTS]
    blocks = w_out.reshape(chans, *sizes, chans).transpose(3, 2, 1, 0, 4)
    split = jnp.einsum(
        "tk,cxzki->cxzti", gated, blocks, preferred_element_type=jnp.float32
    ).astype(jnp.bfloat16)
    for name, size in CH_PARTS[::-1]:
        split = reduced(split, name, size).astype(jnp.bfloat16)
    return split


def solution(mesh):
    shape = [size for _, size in CTX_PARTS] + [size for _, size in CH_PARTS]
    fine = Mesh(mesh.devices.reshape(shape), CTX + CH)
    in_specs = (
        P(CTX, CH),
        P(),
        P(None, None, CH),
        P(None, None, CH),
        P(CH, None),
        P(CH),
        P(CH, None),
    )
    out_specs = P(CTX, CH)
    return jax.shard_map(shards, mesh=fine, in_specs=in_specs, out_specs=out_specs, check_vma=False)
```

```python
import jax
import jax.numpy as jnp
from jax import lax
from jax.experimental import pallas as pl
from jax.experimental.pallas import tpu as pltpu
from jax.sharding import Mesh, PartitionSpec as P

CTX_PARTS = (("z_lo", 4), ("y", 4))
CH_PARTS = (("z_hi", 4), ("x", 4), ("core", 2))
CTX = tuple(name for name, _ in CTX_PARTS)
CH = tuple(name for name, _ in CH_PARTS)
CTX_COUNT = 16
FILTER_ROWS = 64


def passed_along(value, axis, count, steps):
    initial, last = (max(0, -steps), min(count, count - steps))
    return lax.ppermute(value, axis, [(source, source + steps) for source in range(initial, last)])


def gathered(block, name, count):
    copies = jnp.broadcast_to(block[None], (count,) + block.shape)
    return lax.all_to_all(copies, name, 0, 0)


def reduced(stack, name, count):
    parts = lax.all_to_all(stack, name, 0, 0)
    total = parts[0].astype(jnp.float32)
    for member in range(1, count):
        total = total + parts[member].astype(jnp.float32)
    return total


def featurize(extended, feat_taps, count):
    feat_len = feat_taps.shape[1]
    chans = feat_taps.shape[2]
    shaped = extended.reshape(extended.shape[0], 3, chans)
    feats = jnp.zeros((count, 3, chans), jnp.float32)
    for tap in range(feat_len):
        feats = feats + feat_taps[:, tap, :] * shaped[
            feat_len - 1 - tap : feat_len - 1 - tap + count
        ].astype(jnp.float32)
    return feats


def filter_kernel(ext_ref, filt_ref, out_ref, shift_ref):
    taps = filt_ref.shape[0]
    rows = shift_ref.shape[1]
    count = out_ref.shape[0]
    for b in range(8):
        shift_ref[b] = ext_ref[pl.ds(8 - b, rows), :]

    def tile(index, carry):
        base = pl.multiple_of(index * FILTER_ROWS, 8)
        acc = jnp.zeros((FILTER_ROWS, out_ref.shape[1]), jnp.float32)
        for group in range(taps // 8):
            for b in range(8):
                tap = 8 * group + b
                acc = acc + filt_ref[pl.ds(tap, 1), :] * shift_ref[
                    b, pl.ds(base + taps - 8 - 8 * group, FILTER_ROWS), :
                ]
        out_ref[pl.ds(base, FILTER_ROWS), :] = acc
        return carry

    lax.fori_loop(0, count // FILTER_ROWS, tile, 0)


def causal_filter(extended, filt_rows):
    taps, chans = filt_rows.shape
    count = extended.shape[0] - taps
    rows = extended.shape[0] - 8
    return pl.pallas_call(
        filter_kernel,
        out_shape=jax.ShapeDtypeStruct((count, chans), jnp.float32),
        scratch_shapes=[pltpu.VMEM((8, rows, chans), jnp.float32)],
    )(extended, filt_rows)


def shards(bases_in, norm_gain, w_in, feat_taps, long_filter, skip_gain, w_out):
    tok, chans = bases_in.shape
    width = norm_gain.shape[0]
    taps = long_filter.shape[1]
    feat_len = feat_taps.shape[1]
    w_flat = w_in.reshape(width, 3 * chans)
    stacked = lax.all_gather(bases_in, CH[0], axis=0)
    for name, size in CH_PARTS[1:]:
        stacked = gathered(stacked, name, size)
    whole = stacked.transpose(3, 2, 1, 0, 4).reshape(tok, width)
    wide = whole.astype(jnp.float32)
    inverse = lax.rsqrt(jnp.mean(wide * wide, axis=1, keepdims=True) + 1e-05)
    normed = (wide * inverse * norm_gain).astype(jnp.bfloat16)
    mixed_in = jnp.dot(normed, w_flat, preferred_element_type=jnp.float32)
    projected = mixed_in.astype(jnp.bfloat16)
    earlier = passed_along(projected[tok - (taps - 1) - (feat_len - 1) :], CTX, CTX_COUNT, 1)
    early_feats = featurize(earlier, feat_taps, taps - 1)
    before = (early_feats[:, 1, :] * early_feats[:, 2, :]).astype(jnp.bfloat16)
    feats = featurize(
        jnp.concatenate([earlier[earlier.shape[0] - (feat_len - 1) :], projected], axis=0), feat_taps, tok
    )
    query = feats[:, 0, :]
    product = (feats[:, 1, :] * feats[:, 2, :]).astype(jnp.bfloat16)
    extended = jnp.concatenate(
        [jnp.zeros((1, chans), jnp.bfloat16), before, product], axis=0
    ).astype(jnp.float32)
    filtered = causal_filter(extended, long_filter.astype(jnp.float32).T)
    gated = (query * (filtered + skip_gain * product.astype(jnp.float32))).astype(jnp.bfloat16)
    sizes = [size for _, size in CH_PARTS]
    blocks = w_out.reshape(chans, *sizes, chans).transpose(3, 2, 1, 0, 4)
    split = jnp.einsum(
        "tk,cxzki->cxzti", gated, blocks, preferred_element_type=jnp.float32
    ).astype(jnp.bfloat16)
    for name, size in CH_PARTS[::-1]:
        split = reduced(split, name, size).astype(jnp.bfloat16)
    return split


def solution(mesh):
    shape = [size for _, size in CTX_PARTS] + [size for _, size in CH_PARTS]
    fine = Mesh(mesh.devices.reshape(shape), CTX + CH)
    in_specs = (
        P(CTX, CH),
        P(),
        P(None, None, CH),
        P(None, None, CH),
        P(CH, None),
        P(CH),
        P(CH, None),
    )
    out_specs = P(CTX, CH)
    return jax.shard_map(shards, mesh=fine, in_specs=in_specs, out_specs=out_specs, check_vma=False)
```

```python
import jax
import jax.numpy as jnp
from jax import lax
from jax.experimental import pallas as pl
from jax.experimental.pallas import tpu as pltpu
from jax.sharding import Mesh, PartitionSpec as P

CTX_PARTS = (("z_lo", 4), ("y", 4))
CH_PARTS = (("z_hi", 4), ("x", 4), ("core", 2))
CTX = tuple(name for name, _ in CTX_PARTS)
CH = tuple(name for name, _ in CH_PARTS)
CTX_COUNT = 16
FILTER_ROWS = 64


def passed_along(value, axis, count, steps):
    initial, last = (max(0, -steps), min(count, count - steps))
    return lax.ppermute(value, axis, [(source, source + steps) for source in range(initial, last)])


def gathered(block, name, count):
    copies = jnp.broadcast_to(block[None], (count,) + block.shape)
    return lax.all_to_all(copies, name, 0, 0)


def reduced(stack, name, count):
    parts = lax.all_to_all(stack, name, 0, 0)
    total = parts[0].astype(jnp.float32)
    for member in range(1, count):
        total = total + parts[member].astype(jnp.float32)
    return total


def featurize(extended, feat_taps, count):
    feat_len = feat_taps.shape[1]
    chans = feat_taps.shape[2]
    shaped = extended.reshape(extended.shape[0], 3, chans)
    feats = jnp.zeros((count, 3, chans), jnp.float32)
    for tap in range(feat_len):
        feats = feats + feat_taps[:, tap, :] * shaped[
            feat_len - 1 - tap : feat_len - 1 - tap + count
        ].astype(jnp.float32)
    return feats


def filter_kernel(ext_ref, filt_ref, out_ref, shift_ref):
    taps = filt_ref.shape[0]
    rows = shift_ref.shape[1]
    count = out_ref.shape[0]
    for b in range(8):
        shift_ref[b] = ext_ref[pl.ds(8 - b, rows), :]

    def tile(index, carry):
        base = pl.multiple_of(index * FILTER_ROWS, 8)
        acc = jnp.zeros((FILTER_ROWS, out_ref.shape[1]), jnp.float32)
        for group in range(taps // 8):
            for b in range(8):
                tap = 8 * group + b
                acc = acc + filt_ref[pl.ds(tap, 1), :] * shift_ref[
                    b, pl.ds(base + taps - 8 - 8 * group, FILTER_ROWS), :
                ]
        out_ref[pl.ds(base, FILTER_ROWS), :] = acc
        return carry

    lax.fori_loop(0, count // FILTER_ROWS, tile, 0)


def causal_filter(extended, filt_rows):
    taps, chans = filt_rows.shape
    count = extended.shape[0] - taps
    rows = extended.shape[0] - 8
    return pl.pallas_call(
        filter_kernel,
        out_shape=jax.ShapeDtypeStruct((count, chans), jnp.float32),
        scratch_shapes=[pltpu.VMEM((8, rows, chans), jnp.float32)],
    )(extended, filt_rows)


def shards(bases_in, norm_gain, w_in, feat_taps, long_filter, skip_gain, w_out):
    tok, chans = bases_in.shape
    width = norm_gain.shape[0]
    taps = long_filter.shape[1]
    feat_len = feat_taps.shape[1]
    w_flat = w_in.reshape(width, 3 * chans)
    stacked = lax.all_gather(bases_in, CH[0], axis=0)
    for name, size in CH_PARTS[1:]:
        stacked = gathered(stacked, name, size)
    whole = stacked.transpose(3, 2, 1, 0, 4).reshape(tok, width)
    wide = whole.astype(jnp.float32)
    inverse = lax.rsqrt(jnp.mean(wide * wide, axis=1, keepdims=True) + 1e-05)
    normed = (wide * inverse * norm_gain).astype(jnp.bfloat16)
    mixed_in = jnp.dot(normed, w_flat, preferred_element_type=jnp.float32)
    projected = mixed_in.astype(jnp.bfloat16)
    earlier = passed_along(projected[tok - (taps - 1) - (feat_len - 1) :], CTX, CTX_COUNT, 1)
    early_feats = featurize(earlier, feat_taps, taps - 1)
    before = (early_feats[:, 1, :] * early_feats[:, 2, :]).astype(jnp.bfloat16)
    feats = featurize(
        jnp.concatenate([earlier[earlier.shape[0] - (feat_len - 1) :], projected], axis=0), feat_taps, tok
    )
    query = feats[:, 0, :]
    product = (feats[:, 1, :] * feats[:, 2, :]).astype(jnp.bfloat16)
    extended = jnp.concatenate(
        [jnp.zeros((1, chans), jnp.bfloat16), before, product], axis=0
    ).astype(jnp.float32)
    filtered = causal_filter(extended, long_filter.astype(jnp.float32).T)
    gated = (query * (filtered + skip_gain * product.astype(jnp.float32))).astype(jnp.bfloat16)
    sizes = [size for _, size in CH_PARTS]
    blocks = w_out.reshape(chans, *sizes, chans).transpose(3, 2, 1, 0, 4)
    core = lax.axis_index(CH[2])
    mine = lax.dynamic_index_in_dim(blocks, core, 0, keepdims=False)
    theirs = lax.dynamic_index_in_dim(blocks, 1 - core, 0, keepdims=False)
    partner = lambda value: lax.ppermute(value, CH[2], [(0, 1), (1, 0)])
    pair_gated = jnp.concatenate([gated, partner(gated)], axis=1)
    pair_rows = jnp.concatenate([mine, partner(theirs)], axis=2)
    split = jnp.einsum(
        "tk,xzki->xzti", pair_gated, pair_rows, preferred_element_type=jnp.float32
    ).astype(jnp.bfloat16)
    for name, size in CH_PARTS[1::-1]:
        split = reduced(split, name, size).astype(jnp.bfloat16)
    return split


def solution(mesh):
    shape = [size for _, size in CTX_PARTS] + [size for _, size in CH_PARTS]
    fine = Mesh(mesh.devices.reshape(shape), CTX + CH)
    in_specs = (
        P(CTX, CH),
        P(),
        P(None, None, CH),
        P(None, None, CH),
        P(CH, None),
        P(CH),
        P(CH, None),
    )
    out_specs = P(CTX, CH)
    return jax.shard_map(shards, mesh=fine, in_specs=in_specs, out_specs=out_specs, check_vma=False)
```

```python
import jax
import jax.numpy as jnp
from jax import lax
from jax.experimental import pallas as pl
from jax.experimental.pallas import tpu as pltpu
from jax.sharding import Mesh, PartitionSpec as P

CTX_PARTS = (("z_lo", 4), ("y", 4))
CH_PARTS = (("z_hi", 4), ("x", 4), ("core", 2))
CTX = tuple(name for name, _ in CTX_PARTS)
CH = tuple(name for name, _ in CH_PARTS)
CTX_COUNT = 16
FILTER_ROWS = 64


def passed_along(value, axis, count, steps):
    initial, last = (max(0, -steps), min(count, count - steps))
    return lax.ppermute(value, axis, [(source, source + steps) for source in range(initial, last)])


def gathered(block, name, count):
    copies = jnp.broadcast_to(block[None], (count,) + block.shape)
    return lax.all_to_all(copies, name, 0, 0)


def reduced(stack, name, count):
    parts = lax.all_to_all(stack, name, 0, 0)
    total = parts[0].astype(jnp.float32)
    for member in range(1, count):
        total = total + parts[member].astype(jnp.float32)
    return total


def reduced_by_shifts(stack, name, count):
    index = lax.axis_index(name)
    total = lax.dynamic_index_in_dim(stack, index, 0, keepdims=False).astype(jnp.float32)
    for shift in range(1, count):
        part = lax.dynamic_index_in_dim(stack, (index + shift) % count, 0, keepdims=False)
        got = lax.ppermute(part, name, [(k, (k + shift) % count) for k in range(count)])
        total = total + got.astype(jnp.float32)
    return total


def featurize(extended, feat_taps, count):
    feat_len = feat_taps.shape[1]
    chans = feat_taps.shape[2]
    shaped = extended.reshape(extended.shape[0], 3, chans)
    feats = jnp.zeros((count, 3, chans), jnp.float32)
    for tap in range(feat_len):
        feats = feats + feat_taps[:, tap, :] * shaped[
            feat_len - 1 - tap : feat_len - 1 - tap + count
        ].astype(jnp.float32)
    return feats


def filter_kernel(ext_ref, filt_ref, out_ref, shift_ref):
    taps = filt_ref.shape[0]
    rows = shift_ref.shape[1]
    count = out_ref.shape[0]
    for b in range(8):
        shift_ref[b] = ext_ref[pl.ds(8 - b, rows), :]

    def tile(index, carry):
        base = pl.multiple_of(index * FILTER_ROWS, 8)
        acc = jnp.zeros((FILTER_ROWS, out_ref.shape[1]), jnp.float32)
        for group in range(taps // 8):
            for b in range(8):
                tap = 8 * group + b
                acc = acc + filt_ref[pl.ds(tap, 1), :] * shift_ref[
                    b, pl.ds(base + taps - 8 - 8 * group, FILTER_ROWS), :
                ]
        out_ref[pl.ds(base, FILTER_ROWS), :] = acc
        return carry

    lax.fori_loop(0, count // FILTER_ROWS, tile, 0)


def causal_filter(extended, filt_rows):
    taps, chans = filt_rows.shape
    count = extended.shape[0] - taps
    rows = extended.shape[0] - 8
    return pl.pallas_call(
        filter_kernel,
        out_shape=jax.ShapeDtypeStruct((count, chans), jnp.float32),
        scratch_shapes=[pltpu.VMEM((8, rows, chans), jnp.float32)],
    )(extended, filt_rows)


def shards(bases_in, norm_gain, w_in, feat_taps, long_filter, skip_gain, w_out):
    tok, chans = bases_in.shape
    width = norm_gain.shape[0]
    taps = long_filter.shape[1]
    feat_len = feat_taps.shape[1]
    w_flat = w_in.reshape(width, 3 * chans)
    stacked = lax.all_gather(bases_in, CH[0], axis=0)
    for name, size in CH_PARTS[1:]:
        stacked = gathered(stacked, name, size)
    whole = stacked.transpose(3, 2, 1, 0, 4).reshape(tok, width)
    wide = whole.astype(jnp.float32)
    inverse = lax.rsqrt(jnp.mean(wide * wide, axis=1, keepdims=True) + 1e-05)
    normed = (wide * inverse * norm_gain).astype(jnp.bfloat16)
    mixed_in = jnp.dot(normed, w_flat, preferred_element_type=jnp.float32)
    projected = mixed_in.astype(jnp.bfloat16)
    earlier = passed_along(projected[tok - (taps - 1) - (feat_len - 1) :], CTX, CTX_COUNT, 1)
    early_feats = featurize(earlier, feat_taps, taps - 1)
    before = (early_feats[:, 1, :] * early_feats[:, 2, :]).astype(jnp.bfloat16)
    feats = featurize(
        jnp.concatenate([earlier[earlier.shape[0] - (feat_len - 1) :], projected], axis=0), feat_taps, tok
    )
    query = feats[:, 0, :]
    product = (feats[:, 1, :] * feats[:, 2, :]).astype(jnp.bfloat16)
    extended = jnp.concatenate(
        [jnp.zeros((1, chans), jnp.bfloat16), before, product], axis=0
    ).astype(jnp.float32)
    filtered = causal_filter(extended, long_filter.astype(jnp.float32).T)
    gated = (query * (filtered + skip_gain * product.astype(jnp.float32))).astype(jnp.bfloat16)
    sizes = [size for _, size in CH_PARTS]
    blocks = w_out.reshape(chans, *sizes, chans).transpose(3, 2, 1, 0, 4)
    core = lax.axis_index(CH[2])
    mine = lax.dynamic_index_in_dim(blocks, core, 0, keepdims=False)
    theirs = lax.dynamic_index_in_dim(blocks, 1 - core, 0, keepdims=False)
    partner = lambda value: lax.ppermute(value, CH[2], [(0, 1), (1, 0)])
    pair_gated = jnp.concatenate([gated, partner(gated)], axis=1)
    pair_rows = jnp.concatenate([mine, partner(theirs)], axis=2)
    split = jnp.einsum(
        "tk,xzki->xzti", pair_gated, pair_rows, preferred_element_type=jnp.float32
    ).astype(jnp.bfloat16)
    half = tok // 2
    (x_name, x_size), (z_name, z_size) = CH_PARTS[1], CH_PARTS[0]
    first = reduced(split[:, :, :half], x_name, x_size).astype(jnp.bfloat16)
    first, rest = lax.optimization_barrier((first, split[:, :, half:]))
    first = reduced(first, z_name, z_size)
    second = reduced_by_shifts(rest, x_name, x_size).astype(jnp.bfloat16)
    second = reduced(second, z_name, z_size)
    return jnp.concatenate([first, second], axis=0).astype(jnp.bfloat16)


def solution(mesh):
    shape = [size for _, size in CTX_PARTS] + [size for _, size in CH_PARTS]
    fine = Mesh(mesh.devices.reshape(shape), CTX + CH)
    in_specs = (
        P(CTX, CH),
        P(),
        P(None, None, CH),
        P(None, None, CH),
        P(CH, None),
        P(CH),
        P(CH, None),
    )
    out_specs = P(CTX, CH)
    return jax.shard_map(shards, mesh=fine, in_specs=in_specs, out_specs=out_specs, check_vma=False)
```

```python
import jax
import jax.numpy as jnp
from jax import lax
from jax.experimental import pallas as pl
from jax.experimental.pallas import tpu as pltpu
from jax.sharding import Mesh, PartitionSpec as P

CTX_PARTS = (("z_lo", 4), ("y", 4))
CH_PARTS = (("z_hi", 4), ("x", 4), ("core", 2))
CTX = tuple(name for name, _ in CTX_PARTS)
CH = tuple(name for name, _ in CH_PARTS)
CTX_COUNT = 16
FILTER_ROWS = 64


def passed_along(value, axis, count, steps):
    initial, last = (max(0, -steps), min(count, count - steps))
    return lax.ppermute(value, axis, [(source, source + steps) for source in range(initial, last)])


def gathered(block, name, count):
    copies = jnp.broadcast_to(block[None], (count,) + block.shape)
    return lax.all_to_all(copies, name, 0, 0)


def reduced(stack, name, count):
    parts = lax.all_to_all(stack, name, 0, 0)
    total = parts[0].astype(jnp.float32)
    for member in range(1, count):
        total = total + parts[member].astype(jnp.float32)
    return total


def featurize(extended, feat_taps, count):
    feat_len = feat_taps.shape[1]
    chans = feat_taps.shape[2]
    shaped = extended.reshape(extended.shape[0], 3, chans)
    feats = jnp.zeros((count, 3, chans), jnp.float32)
    for tap in range(feat_len):
        feats = feats + feat_taps[:, tap, :] * shaped[
            feat_len - 1 - tap : feat_len - 1 - tap + count
        ].astype(jnp.float32)
    return feats


def filter_kernel(ext_ref, filt_ref, out_ref, shift_ref):
    taps = filt_ref.shape[0]
    rows = shift_ref.shape[1]
    count = out_ref.shape[0]
    for b in range(8):
        shift_ref[b] = ext_ref[pl.ds(8 - b, rows), :]

    def tile(index, carry):
        base = pl.multiple_of(index * FILTER_ROWS, 8)
        acc = jnp.zeros((FILTER_ROWS, out_ref.shape[1]), jnp.float32)
        for group in range(taps // 8):
            for b in range(8):
                tap = 8 * group + b
                acc = acc + filt_ref[pl.ds(tap, 1), :] * shift_ref[
                    b, pl.ds(base + taps - 8 - 8 * group, FILTER_ROWS), :
                ]
        out_ref[pl.ds(base, FILTER_ROWS), :] = acc
        return carry

    lax.fori_loop(0, count // FILTER_ROWS, tile, 0)


def causal_filter(extended, filt_rows):
    taps, chans = filt_rows.shape
    count = extended.shape[0] - taps
    rows = extended.shape[0] - 8
    return pl.pallas_call(
        filter_kernel,
        out_shape=jax.ShapeDtypeStruct((count, chans), jnp.float32),
        scratch_shapes=[pltpu.VMEM((8, rows, chans), jnp.float32)],
    )(extended, filt_rows)


def shards(bases_in, norm_gain, w_in, feat_taps, long_filter, skip_gain, w_out):
    tok, chans = bases_in.shape
    width = norm_gain.shape[0]
    taps = long_filter.shape[1]
    feat_len = feat_taps.shape[1]
    w_flat = w_in.reshape(width, 3 * chans)
    stacked = lax.all_gather(bases_in, CH[0], axis=0)
    for name, size in CH_PARTS[1:]:
        stacked = gathered(stacked, name, size)
    whole = stacked.transpose(3, 2, 1, 0, 4).reshape(tok, width)
    wide = whole.astype(jnp.float32)
    inverse = lax.rsqrt(jnp.mean(wide * wide, axis=1, keepdims=True) + 1e-05)
    normed = (wide * inverse * norm_gain).astype(jnp.bfloat16)
    mixed_in = jnp.dot(normed, w_flat, preferred_element_type=jnp.float32)
    projected = mixed_in.astype(jnp.bfloat16)
    earlier = passed_along(projected[tok - (taps - 1) - (feat_len - 1) :], CTX, CTX_COUNT, 1)
    local_feats = featurize(projected, feat_taps, tok - (feat_len - 1))
    local_product = (local_feats[:, 1, :] * local_feats[:, 2, :]).astype(jnp.bfloat16)
    filt_rows = long_filter.astype(jnp.float32).T
    half = tok // 2
    tail = causal_filter(local_product[half - taps - (feat_len - 1) :].astype(jnp.float32), filt_rows)
    tail, earlier = lax.optimization_barrier((tail, earlier))
    early_feats = featurize(earlier, feat_taps, taps - 1)
    before = (early_feats[:, 1, :] * early_feats[:, 2, :]).astype(jnp.bfloat16)
    head_feats = featurize(
        jnp.concatenate([earlier[earlier.shape[0] - (feat_len - 1) :], projected[: feat_len - 1]], axis=0),
        feat_taps,
        feat_len - 1,
    )
    query = jnp.concatenate([head_feats[:, 0, :], local_feats[:, 0, :]], axis=0)
    head_product = (head_feats[:, 1, :] * head_feats[:, 2, :]).astype(jnp.bfloat16)
    product = jnp.concatenate([head_product, local_product], axis=0)
    head = causal_filter(
        jnp.concatenate([jnp.zeros((1, chans), jnp.bfloat16), before, product[:half]], axis=0).astype(jnp.float32),
        filt_rows,
    )
    filtered = jnp.concatenate([head, tail], axis=0)
    gated = (query * (filtered + skip_gain * product.astype(jnp.float32))).astype(jnp.bfloat16)
    sizes = [size for _, size in CH_PARTS]
    blocks = w_out.reshape(chans, *sizes, chans).transpose(3, 2, 1, 0, 4)
    core = lax.axis_index(CH[2])
    mine = lax.dynamic_index_in_dim(blocks, core, 0, keepdims=False)
    theirs = lax.dynamic_index_in_dim(blocks, 1 - core, 0, keepdims=False)
    partner = lambda value: lax.ppermute(value, CH[2], [(0, 1), (1, 0)])
    own_part = jnp.einsum("tk,xzki->xzti", gated, mine, preferred_element_type=jnp.float32)
    their_part = jnp.einsum(
        "tk,xzki->xzti", partner(gated), partner(theirs), preferred_element_type=jnp.float32
    )
    split = (own_part + their_part).astype(jnp.bfloat16)
    for name, size in CH_PARTS[1::-1]:
        split = reduced(split, name, size).astype(jnp.bfloat16)
    return split


def solution(mesh):
    shape = [size for _, size in CTX_PARTS] + [size for _, size in CH_PARTS]
    fine = Mesh(mesh.devices.reshape(shape), CTX + CH)
    in_specs = (
        P(CTX, CH),
        P(),
        P(None, None, CH),
        P(None, None, CH),
        P(CH, None),
        P(CH),
        P(CH, None),
    )
    out_specs = P(CTX, CH)
    return jax.shard_map(shards, mesh=fine, in_specs=in_specs, out_specs=out_specs, check_vma=False)
```

```python
import jax
import jax.numpy as jnp
from jax import lax
from jax.experimental import pallas as pl
from jax.experimental.pallas import tpu as pltpu
from jax.sharding import Mesh, PartitionSpec as P

CTX_PARTS = (("z_lo", 4), ("y", 4))
CH_PARTS = (("z_hi", 4), ("x", 4), ("core", 2))
CTX = tuple(name for name, _ in CTX_PARTS)
CH = tuple(name for name, _ in CH_PARTS)
CTX_COUNT = 16
FILTER_ROWS = 64


def passed_along(value, axis, count, steps):
    initial, last = (max(0, -steps), min(count, count - steps))
    return lax.ppermute(value, axis, [(source, source + steps) for source in range(initial, last)])


def gathered(block, name, count):
    copies = jnp.broadcast_to(block[None], (count,) + block.shape)
    return lax.all_to_all(copies, name, 0, 0)


def reduced(stack, name, count):
    parts = lax.all_to_all(stack, name, 0, 0)
    total = parts[0].astype(jnp.float32)
    for member in range(1, count):
        total = total + parts[member].astype(jnp.float32)
    return total


def featurize(extended, feat_taps, count):
    feat_len = feat_taps.shape[1]
    chans = feat_taps.shape[2]
    shaped = extended.reshape(extended.shape[0], 3, chans)
    feats = jnp.zeros((count, 3, chans), jnp.float32)
    for tap in range(feat_len):
        feats = feats + feat_taps[:, tap, :] * shaped[
            feat_len - 1 - tap : feat_len - 1 - tap + count
        ].astype(jnp.float32)
    return feats


def filter_kernel(ext_ref, filt_ref, query_ref, skip_ref, out_ref, wide_ref, shift_ref):
    taps = filt_ref.shape[0]
    rows = shift_ref.shape[1]
    count = out_ref.shape[0]
    wide_ref[...] = ext_ref[...].astype(jnp.float32)
    for b in range(8):
        shift_ref[b] = wide_ref[pl.ds(8 - b, rows), :]

    def tile(index, carry):
        base = pl.multiple_of(index * FILTER_ROWS, 8)
        acc = jnp.zeros((FILTER_ROWS, out_ref.shape[1]), jnp.float32)
        for group in range(taps // 8):
            for b in range(8):
                tap = 8 * group + b
                acc = acc + filt_ref[pl.ds(tap, 1), :] * shift_ref[
                    b, pl.ds(base + taps - 8 - 8 * group, FILTER_ROWS), :
                ]
        own = wide_ref[pl.ds(base + taps, FILTER_ROWS), :]
        query = query_ref[pl.ds(base, FILTER_ROWS), :]
        out_ref[pl.ds(base, FILTER_ROWS), :] = (query * (acc + skip_ref[...] * own)).astype(out_ref.dtype)
        return carry

    lax.fori_loop(0, count // FILTER_ROWS, tile, 0)


def gated_filter(extended, filt_rows, query, skip):
    taps, chans = filt_rows.shape
    count = extended.shape[0] - taps
    rows = extended.shape[0] - 8
    return pl.pallas_call(
        filter_kernel,
        out_shape=jax.ShapeDtypeStruct((count, chans), jnp.bfloat16),
        scratch_shapes=[
            pltpu.VMEM((extended.shape[0], chans), jnp.float32),
            pltpu.VMEM((8, rows, chans), jnp.float32),
        ],
    )(extended, filt_rows, query, skip.reshape(1, chans))


def shards(bases_in, norm_gain, w_in, feat_taps, long_filter, skip_gain, w_out):
    tok, chans = bases_in.shape
    width = norm_gain.shape[0]
    taps = long_filter.shape[1]
    feat_len = feat_taps.shape[1]
    w_flat = w_in.reshape(width, 3 * chans)
    stacked = lax.all_gather(bases_in, CH[0], axis=0)
    for name, size in CH_PARTS[1:]:
        stacked = gathered(stacked, name, size)
    whole = stacked.transpose(3, 2, 1, 0, 4).reshape(tok, width)
    wide = whole.astype(jnp.float32)
    inverse = lax.rsqrt(jnp.mean(wide * wide, axis=1, keepdims=True) + 1e-05)
    normed = (wide * inverse * norm_gain).astype(jnp.bfloat16)
    mixed_in = jnp.dot(normed, w_flat, preferred_element_type=jnp.float32)
    projected = mixed_in.astype(jnp.bfloat16)
    earlier = passed_along(projected[tok - (taps - 1) - (feat_len - 1) :], CTX, CTX_COUNT, 1)
    local_feats = featurize(projected, feat_taps, tok - (feat_len - 1))
    local_product = (local_feats[:, 1, :] * local_feats[:, 2, :]).astype(jnp.bfloat16)
    filt_rows = long_filter.astype(jnp.float32).T
    half = tok // 2
    local_query = local_feats[:, 0, :]
    tail = gated_filter(
        local_product[half - taps - (feat_len - 1) :], filt_rows, local_query[half - (feat_len - 1) :], skip_gain
    )
    tail, earlier = lax.optimization_barrier((tail, earlier))
    early_feats = featurize(earlier, feat_taps, taps - 1)
    before = (early_feats[:, 1, :] * early_feats[:, 2, :]).astype(jnp.bfloat16)
    head_feats = featurize(
        jnp.concatenate([earlier[earlier.shape[0] - (feat_len - 1) :], projected[: feat_len - 1]], axis=0),
        feat_taps,
        feat_len - 1,
    )
    query = jnp.concatenate([head_feats[:, 0, :], local_query], axis=0)
    head_product = (head_feats[:, 1, :] * head_feats[:, 2, :]).astype(jnp.bfloat16)
    product = jnp.concatenate([head_product, local_product], axis=0)
    head = gated_filter(
        jnp.concatenate([jnp.zeros((1, chans), jnp.bfloat16), before, product[:half]], axis=0),
        filt_rows,
        query[:half],
        skip_gain,
    )
    gated = jnp.concatenate([head, tail], axis=0)
    sizes = [size for _, size in CH_PARTS]
    blocks = w_out.reshape(chans, *sizes, chans).transpose(3, 2, 1, 0, 4)
    core = lax.axis_index(CH[2])
    mine = lax.dynamic_index_in_dim(blocks, core, 0, keepdims=False)
    theirs = lax.dynamic_index_in_dim(blocks, 1 - core, 0, keepdims=False)
    partner = lambda value: lax.ppermute(value, CH[2], [(0, 1), (1, 0)])
    own_part = jnp.einsum("tk,xzki->xzti", gated, mine, preferred_element_type=jnp.float32)
    their_part = jnp.einsum(
        "tk,xzki->xzti", partner(gated), partner(theirs), preferred_element_type=jnp.float32
    )
    split = (own_part + their_part).astype(jnp.bfloat16)
    for name, size in CH_PARTS[1::-1]:
        split = reduced(split, name, size).astype(jnp.bfloat16)
    return split


def solution(mesh):
    shape = [size for _, size in CTX_PARTS] + [size for _, size in CH_PARTS]
    fine = Mesh(mesh.devices.reshape(shape), CTX + CH)
    in_specs = (
        P(CTX, CH),
        P(),
        P(None, None, CH),
        P(None, None, CH),
        P(CH, None),
        P(CH),
        P(CH, None),
    )
    out_specs = P(CTX, CH)
    return jax.shard_map(shards, mesh=fine, in_specs=in_specs, out_specs=out_specs, check_vma=False)
```

```python
import jax
import jax.numpy as jnp
from jax import lax
from jax.experimental import pallas as pl
from jax.experimental.pallas import tpu as pltpu
from jax.sharding import Mesh, PartitionSpec as P

CTX_PARTS = (("z_lo", 4), ("y", 4))
CH_PARTS = (("z_hi", 4), ("x", 4), ("core", 2))
CTX = tuple(name for name, _ in CTX_PARTS)
CH = tuple(name for name, _ in CH_PARTS)
CTX_COUNT = 16
FILTER_ROWS = 64


def passed_along(value, axis, count, steps):
    initial, last = (max(0, -steps), min(count, count - steps))
    return lax.ppermute(value, axis, [(source, source + steps) for source in range(initial, last)])


def gathered(block, name, count):
    if count == 2:
        index = lax.axis_index(name)
        other = lax.ppermute(block, name, [(0, 1), (1, 0)])
        return jnp.where(index == 0, jnp.stack([block, other]), jnp.stack([other, block]))
    copies = jnp.broadcast_to(block[None], (count,) + block.shape)
    return lax.all_to_all(copies, name, 0, 0)


def reduced(stack, name, count):
    parts = lax.all_to_all(stack, name, 0, 0)
    total = parts[0].astype(jnp.float32)
    for member in range(1, count):
        total = total + parts[member].astype(jnp.float32)
    return total


def featurize(extended, feat_taps, count):
    feat_len = feat_taps.shape[1]
    chans = feat_taps.shape[2]
    shaped = extended.reshape(extended.shape[0], 3, chans)
    feats = jnp.zeros((count, 3, chans), jnp.float32)
    for tap in range(feat_len):
        feats = feats + feat_taps[:, tap, :] * shaped[
            feat_len - 1 - tap : feat_len - 1 - tap + count
        ].astype(jnp.float32)
    return feats


def filter_kernel(ext_ref, filt_ref, out_ref, shift_ref):
    taps = filt_ref.shape[0]
    rows = shift_ref.shape[1]
    count = out_ref.shape[0]
    for b in range(8):
        shift_ref[b] = ext_ref[pl.ds(8 - b, rows), :]

    def tile(index, carry):
        base = pl.multiple_of(index * FILTER_ROWS, 8)
        acc = jnp.zeros((FILTER_ROWS, out_ref.shape[1]), jnp.float32)
        for group in range(taps // 8):
            for b in range(8):
                tap = 8 * group + b
                acc = acc + filt_ref[pl.ds(tap, 1), :] * shift_ref[
                    b, pl.ds(base + taps - 8 - 8 * group, FILTER_ROWS), :
                ]
        out_ref[pl.ds(base, FILTER_ROWS), :] = acc
        return carry

    lax.fori_loop(0, count // FILTER_ROWS, tile, 0)


def causal_filter(extended, filt_rows):
    taps, chans = filt_rows.shape
    count = extended.shape[0] - taps
    rows = extended.shape[0] - 8
    return pl.pallas_call(
        filter_kernel,
        out_shape=jax.ShapeDtypeStruct((count, chans), jnp.float32),
        scratch_shapes=[pltpu.VMEM((8, rows, chans), jnp.float32)],
    )(extended, filt_rows)


def shards(bases_in, norm_gain, w_in, feat_taps, long_filter, skip_gain, w_out):
    tok, chans = bases_in.shape
    width = norm_gain.shape[0]
    taps = long_filter.shape[1]
    feat_len = feat_taps.shape[1]
    w_flat = w_in.reshape(width, 3 * chans)
    stacked = lax.all_gather(bases_in, CH[0], axis=0)
    for name, size in CH_PARTS[1:]:
        stacked = gathered(stacked, name, size)
    whole = stacked.transpose(3, 2, 1, 0, 4).reshape(tok, width)
    wide = whole.astype(jnp.float32)
    inverse = lax.rsqrt(jnp.mean(wide * wide, axis=1, keepdims=True) + 1e-05)
    normed = (wide * inverse * norm_gain).astype(jnp.bfloat16)
    mixed_in = jnp.dot(normed, w_flat, preferred_element_type=jnp.float32)
    projected = mixed_in.astype(jnp.bfloat16)
    earlier = passed_along(projected[tok - (taps - 1) - (feat_len - 1) :], CTX, CTX_COUNT, 1)
    local_feats = featurize(projected, feat_taps, tok - (feat_len - 1))
    local_product = (local_feats[:, 1, :] * local_feats[:, 2, :]).astype(jnp.bfloat16)
    filt_rows = long_filter.astype(jnp.float32).T
    half = tok // 2
    tail = causal_filter(local_product[half - taps - (feat_len - 1) :].astype(jnp.float32), filt_rows)
    tail, earlier = lax.optimization_barrier((tail, earlier))
    early_feats = featurize(earlier, feat_taps, taps - 1)
    before = (early_feats[:, 1, :] * early_feats[:, 2, :]).astype(jnp.bfloat16)
    head_feats = featurize(
        jnp.concatenate([earlier[earlier.shape[0] - (feat_len - 1) :], projected[: feat_len - 1]], axis=0),
        feat_taps,
        feat_len - 1,
    )
    query = jnp.concatenate([head_feats[:, 0, :], local_feats[:, 0, :]], axis=0)
    head_product = (head_feats[:, 1, :] * head_feats[:, 2, :]).astype(jnp.bfloat16)
    product = jnp.concatenate([head_product, local_product], axis=0)
    head = causal_filter(
        jnp.concatenate([jnp.zeros((1, chans), jnp.bfloat16), before, product[:half]], axis=0).astype(jnp.float32),
        filt_rows,
    )
    filtered = jnp.concatenate([head, tail], axis=0)
    gated = (query * (filtered + skip_gain * product.astype(jnp.float32))).astype(jnp.bfloat16)
    sizes = [size for _, size in CH_PARTS]
    blocks = w_out.reshape(chans, *sizes, chans).transpose(3, 2, 1, 0, 4)
    core = lax.axis_index(CH[2])
    mine = lax.dynamic_index_in_dim(blocks, core, 0, keepdims=False)
    theirs = lax.dynamic_index_in_dim(blocks, 1 - core, 0, keepdims=False)
    partner = lambda value: lax.ppermute(value, CH[2], [(0, 1), (1, 0)])
    own_part = jnp.einsum("tk,xzki->xzti", gated, mine, preferred_element_type=jnp.float32)
    their_part = jnp.einsum(
        "tk,xzki->xzti", partner(gated), partner(theirs), preferred_element_type=jnp.float32
    )
    split = (own_part + their_part).astype(jnp.bfloat16)
    for name, size in CH_PARTS[1::-1]:
        split = reduced(split, name, size).astype(jnp.bfloat16)
    return split


def solution(mesh):
    shape = [size for _, size in CTX_PARTS] + [size for _, size in CH_PARTS]
    fine = Mesh(mesh.devices.reshape(shape), CTX + CH)
    in_specs = (
        P(CTX, CH),
        P(),
        P(None, None, CH),
        P(None, None, CH),
        P(CH, None),
        P(CH),
        P(CH, None),
    )
    out_specs = P(CTX, CH)
    return jax.shard_map(shards, mesh=fine, in_specs=in_specs, out_specs=out_specs, check_vma=False)
```

```python
import jax
import jax.numpy as jnp
from jax import lax
from jax.experimental import pallas as pl
from jax.experimental.pallas import tpu as pltpu
from jax.sharding import Mesh, PartitionSpec as P

CTX_PARTS = (("z_lo", 4), ("y", 4))
CH_PARTS = (("z_hi", 4), ("x", 4), ("core", 2))
CTX = tuple(name for name, _ in CTX_PARTS)
CH = tuple(name for name, _ in CH_PARTS)
CTX_COUNT = 16
FILTER_ROWS = 32


def passed_along(value, axis, count, steps):
    initial, last = (max(0, -steps), min(count, count - steps))
    return lax.ppermute(value, axis, [(source, source + steps) for source in range(initial, last)])


def gathered(block, name, count):
    copies = jnp.broadcast_to(block[None], (count,) + block.shape)
    return lax.all_to_all(copies, name, 0, 0)


def reduced(stack, name, count):
    parts = lax.all_to_all(stack, name, 0, 0)
    total = parts[0].astype(jnp.float32)
    for member in range(1, count):
        total = total + parts[member].astype(jnp.float32)
    return total


def featurize(extended, feat_taps, count):
    feat_len = feat_taps.shape[1]
    chans = feat_taps.shape[2]
    shaped = extended.reshape(extended.shape[0], 3, chans)
    feats = jnp.zeros((count, 3, chans), jnp.float32)
    for tap in range(feat_len):
        feats = feats + feat_taps[:, tap, :] * shaped[
            feat_len - 1 - tap : feat_len - 1 - tap + count
        ].astype(jnp.float32)
    return feats


def filter_kernel(ext_ref, filt_ref, out_ref, shift_ref):
    taps = filt_ref.shape[0]
    rows = shift_ref.shape[1]
    count = out_ref.shape[0]
    for b in range(8):
        shift_ref[b] = ext_ref[pl.ds(8 - b, rows), :]

    def tile(index, carry):
        base = pl.multiple_of(index * FILTER_ROWS, 8)
        acc = jnp.zeros((FILTER_ROWS, out_ref.shape[1]), jnp.float32)
        for group in range(taps // 8):
            for b in range(8):
                tap = 8 * group + b
                acc = acc + filt_ref[pl.ds(tap, 1), :] * shift_ref[
                    b, pl.ds(base + taps - 8 - 8 * group, FILTER_ROWS), :
                ]
        out_ref[pl.ds(base, FILTER_ROWS), :] = acc
        return carry

    lax.fori_loop(0, count // FILTER_ROWS, tile, 0)


def causal_filter(extended, filt_rows):
    taps, chans = filt_rows.shape
    count = extended.shape[0] - taps
    rows = extended.shape[0] - 8
    return pl.pallas_call(
        filter_kernel,
        out_shape=jax.ShapeDtypeStruct((count, chans), jnp.float32),
        scratch_shapes=[pltpu.VMEM((8, rows, chans), jnp.float32)],
    )(extended, filt_rows)


def shards(bases_in, norm_gain, w_in, feat_taps, long_filter, skip_gain, w_out):
    tok, chans = bases_in.shape
    width = norm_gain.shape[0]
    taps = long_filter.shape[1]
    feat_len = feat_taps.shape[1]
    w_flat = w_in.reshape(width, 3 * chans)
    stacked = lax.all_gather(bases_in, CH[0], axis=0)
    for name, size in CH_PARTS[1:]:
        stacked = gathered(stacked, name, size)
    whole = stacked.transpose(3, 2, 1, 0, 4).reshape(tok, width)
    wide = whole.astype(jnp.float32)
    inverse = lax.rsqrt(jnp.mean(wide * wide, axis=1, keepdims=True) + 1e-05)
    normed = (wide * inverse * norm_gain).astype(jnp.bfloat16)
    mixed_in = jnp.dot(normed, w_flat, preferred_element_type=jnp.float32)
    projected = mixed_in.astype(jnp.bfloat16)
    earlier = passed_along(projected[tok - (taps - 1) - (feat_len - 1) :], CTX, CTX_COUNT, 1)
    local_feats = featurize(projected, feat_taps, tok - (feat_len - 1))
    local_product = (local_feats[:, 1, :] * local_feats[:, 2, :]).astype(jnp.bfloat16)
    filt_rows = long_filter.astype(jnp.float32).T
    half = taps + 32
    tail = causal_filter(local_product[half - taps - (feat_len - 1) :].astype(jnp.float32), filt_rows)
    tail, earlier = lax.optimization_barrier((tail, earlier))
    early_feats = featurize(earlier, feat_taps, taps - 1)
    before = (early_feats[:, 1, :] * early_feats[:, 2, :]).astype(jnp.bfloat16)
    head_feats = featurize(
        jnp.concatenate([earlier[earlier.shape[0] - (feat_len - 1) :], projected[: feat_len - 1]], axis=0),
        feat_taps,
        feat_len - 1,
    )
    query = jnp.concatenate([head_feats[:, 0, :], local_feats[:, 0, :]], axis=0)
    head_product = (head_feats[:, 1, :] * head_feats[:, 2, :]).astype(jnp.bfloat16)
    product = jnp.concatenate([head_product, local_product], axis=0)
    head = causal_filter(
        jnp.concatenate([jnp.zeros((1, chans), jnp.bfloat16), before, product[:half]], axis=0).astype(jnp.float32),
        filt_rows,
    )
    filtered = jnp.concatenate([head, tail], axis=0)
    gated = (query * (filtered + skip_gain * product.astype(jnp.float32))).astype(jnp.bfloat16)
    sizes = [size for _, size in CH_PARTS]
    blocks = w_out.reshape(chans, *sizes, chans).transpose(3, 2, 1, 0, 4)
    core = lax.axis_index(CH[2])
    mine = lax.dynamic_index_in_dim(blocks, core, 0, keepdims=False)
    theirs = lax.dynamic_index_in_dim(blocks, 1 - core, 0, keepdims=False)
    partner = lambda value: lax.ppermute(value, CH[2], [(0, 1), (1, 0)])
    own_part = jnp.einsum("tk,xzki->xzti", gated, mine, preferred_element_type=jnp.float32)
    their_part = jnp.einsum(
        "tk,xzki->xzti", partner(gated), partner(theirs), preferred_element_type=jnp.float32
    )
    split = (own_part + their_part).astype(jnp.bfloat16)
    for name, size in CH_PARTS[1::-1]:
        split = reduced(split, name, size).astype(jnp.bfloat16)
    return split


def solution(mesh):
    shape = [size for _, size in CTX_PARTS] + [size for _, size in CH_PARTS]
    fine = Mesh(mesh.devices.reshape(shape), CTX + CH)
    in_specs = (
        P(CTX, CH),
        P(),
        P(None, None, CH),
        P(None, None, CH),
        P(CH, None),
        P(CH),
        P(CH, None),
    )
    out_specs = P(CTX, CH)
    return jax.shard_map(shards, mesh=fine, in_specs=in_specs, out_specs=out_specs, check_vma=False)
```

```python
import jax
import jax.numpy as jnp
from jax import lax
from jax.experimental import pallas as pl
from jax.experimental.pallas import tpu as pltpu
from jax.sharding import Mesh, PartitionSpec as P

CTX_PARTS = (("z_lo", 4), ("y", 4))
CH_PARTS = (("z_hi", 4), ("x", 4), ("core", 2))
CTX = tuple(name for name, _ in CTX_PARTS)
CH = tuple(name for name, _ in CH_PARTS)
CTX_COUNT = 16
FILTER_ROWS = 64


def passed_along(value, axis, count, steps):
    initial, last = (max(0, -steps), min(count, count - steps))
    return lax.ppermute(value, axis, [(source, source + steps) for source in range(initial, last)])


def gathered(block, name, count):
    copies = jnp.broadcast_to(block[None], (count,) + block.shape)
    return lax.all_to_all(copies, name, 0, 0)


def reduced(stack, name, count):
    parts = lax.all_to_all(stack, name, 0, 0)
    total = parts[0].astype(jnp.float32)
    for member in range(1, count):
        total = total + parts[member].astype(jnp.float32)
    return total


def featurize(extended, feat_taps, count):
    feat_len = feat_taps.shape[1]
    chans = feat_taps.shape[2]
    shaped = extended.reshape(extended.shape[0], 3, chans)
    feats = jnp.zeros((count, 3, chans), jnp.float32)
    for tap in range(feat_len):
        feats = feats + feat_taps[:, tap, :] * shaped[
            feat_len - 1 - tap : feat_len - 1 - tap + count
        ].astype(jnp.float32)
    return feats


def filter_kernel(ext_ref, filt_ref, out_ref, shift_ref):
    taps = filt_ref.shape[0]
    rows = shift_ref.shape[1]
    count = out_ref.shape[0]
    for b in range(8):
        shift_ref[b] = ext_ref[pl.ds(8 - b, rows), :]

    def tile(index, carry):
        base = pl.multiple_of(index * FILTER_ROWS, 8)
        acc = jnp.zeros((FILTER_ROWS, out_ref.shape[1]), jnp.float32)
        for group in range(taps // 8):
            for b in range(8):
                tap = 8 * group + b
                acc = acc + filt_ref[pl.ds(tap, 1), :] * shift_ref[
                    b, pl.ds(base + taps - 8 - 8 * group, FILTER_ROWS), :
                ]
        out_ref[pl.ds(base, FILTER_ROWS), :] = acc
        return carry

    lax.fori_loop(0, count // FILTER_ROWS, tile, 0)


def causal_filter(extended, filt_rows):
    taps, chans = filt_rows.shape
    count = extended.shape[0] - taps
    rows = extended.shape[0] - 8
    return pl.pallas_call(
        filter_kernel,
        out_shape=jax.ShapeDtypeStruct((count, chans), jnp.float32),
        scratch_shapes=[pltpu.VMEM((8, rows, chans), jnp.float32)],
    )(extended, filt_rows)


def norm_kernel(xs_ref, gain_ref, w_ref, out_ref, normed_ref):
    blocks, _, chans = xs_ref.shape
    total = jnp.zeros((xs_ref.shape[1], 1), jnp.float32)
    for b in range(blocks):
        wide = xs_ref[b].astype(jnp.float32)
        total = total + jnp.sum(wide * wide, axis=1, keepdims=True)
    inverse = lax.rsqrt(total / (blocks * chans) + 1e-05)
    for b in range(blocks):
        wide = xs_ref[b].astype(jnp.float32)
        normed_ref[:, b * chans : (b + 1) * chans] = (wide * inverse * gain_ref[pl.ds(b, 1), :]).astype(jnp.bfloat16)
    out_ref[...] = jnp.dot(normed_ref[...], w_ref[...], preferred_element_type=jnp.float32).astype(out_ref.dtype)


def normed_projection(xs, gain, w):
    blocks, tok, chans = xs.shape
    return pl.pallas_call(
        norm_kernel,
        out_shape=jax.ShapeDtypeStruct((tok, w.shape[1]), jnp.bfloat16),
        scratch_shapes=[pltpu.VMEM((tok, blocks * chans), jnp.bfloat16)],
    )(xs, gain, w)


def shards(bases_in, norm_gain, w_in, feat_taps, long_filter, skip_gain, w_out):
    tok, chans = bases_in.shape
    width = norm_gain.shape[0]
    taps = long_filter.shape[1]
    feat_len = feat_taps.shape[1]
    w_flat = w_in.reshape(width, 3 * chans)
    stacked = lax.all_gather(bases_in, CH[0], axis=0)
    for name, size in CH_PARTS[1:]:
        stacked = gathered(stacked, name, size)
    sizes = [size for _, size in CH_PARTS]
    order = lambda value: value.reshape(*sizes, chans, *value.shape[1:]).transpose(2, 1, 0, *range(3, value.ndim + 3))
    xs = stacked.reshape(-1, tok, chans)
    gain = order(norm_gain).reshape(-1, chans)
    w_rows = order(w_flat).reshape(width, 3 * chans)
    projected = normed_projection(xs, gain, w_rows)
    earlier = passed_along(projected[tok - (taps - 1) - (feat_len - 1) :], CTX, CTX_COUNT, 1)
    local_feats = featurize(projected, feat_taps, tok - (feat_len - 1))
    local_product = (local_feats[:, 1, :] * local_feats[:, 2, :]).astype(jnp.bfloat16)
    filt_rows = long_filter.astype(jnp.float32).T
    half = tok // 2
    tail = causal_filter(local_product[half - taps - (feat_len - 1) :].astype(jnp.float32), filt_rows)
    tail, earlier = lax.optimization_barrier((tail, earlier))
    early_feats = featurize(earlier, feat_taps, taps - 1)
    before = (early_feats[:, 1, :] * early_feats[:, 2, :]).astype(jnp.bfloat16)
    head_feats = featurize(
        jnp.concatenate([earlier[earlier.shape[0] - (feat_len - 1) :], projected[: feat_len - 1]], axis=0),
        feat_taps,
        feat_len - 1,
    )
    query = jnp.concatenate([head_feats[:, 0, :], local_feats[:, 0, :]], axis=0)
    head_product = (head_feats[:, 1, :] * head_feats[:, 2, :]).astype(jnp.bfloat16)
    product = jnp.concatenate([head_product, local_product], axis=0)
    head = causal_filter(
        jnp.concatenate([jnp.zeros((1, chans), jnp.bfloat16), before, product[:half]], axis=0).astype(jnp.float32),
        filt_rows,
    )
    filtered = jnp.concatenate([head, tail], axis=0)
    gated = (query * (filtered + skip_gain * product.astype(jnp.float32))).astype(jnp.bfloat16)
    sizes = [size for _, size in CH_PARTS]
    blocks = w_out.reshape(chans, *sizes, chans).transpose(3, 2, 1, 0, 4)
    core = lax.axis_index(CH[2])
    mine = lax.dynamic_index_in_dim(blocks, core, 0, keepdims=False)
    theirs = lax.dynamic_index_in_dim(blocks, 1 - core, 0, keepdims=False)
    partner = lambda value: lax.ppermute(value, CH[2], [(0, 1), (1, 0)])
    own_part = jnp.einsum("tk,xzki->xzti", gated, mine, preferred_element_type=jnp.float32)
    their_part = jnp.einsum(
        "tk,xzki->xzti", partner(gated), partner(theirs), preferred_element_type=jnp.float32
    )
    split = (own_part + their_part).astype(jnp.bfloat16)
    for name, size in CH_PARTS[1::-1]:
        split = reduced(split, name, size).astype(jnp.bfloat16)
    return split


def solution(mesh):
    shape = [size for _, size in CTX_PARTS] + [size for _, size in CH_PARTS]
    fine = Mesh(mesh.devices.reshape(shape), CTX + CH)
    in_specs = (
        P(CTX, CH),
        P(),
        P(None, None, CH),
        P(None, None, CH),
        P(CH, None),
        P(CH),
        P(CH, None),
    )
    out_specs = P(CTX, CH)
    return jax.shard_map(shards, mesh=fine, in_specs=in_specs, out_specs=out_specs, check_vma=False)
```

```python
import jax
import jax.numpy as jnp
from jax import lax
from jax.experimental import pallas as pl
from jax.experimental.pallas import tpu as pltpu
from jax.sharding import Mesh, PartitionSpec as P

CTX_PARTS = (("z_lo", 4), ("y", 4))
CH_PARTS = (("z_hi", 4), ("x", 4), ("core", 2))
CTX = tuple(name for name, _ in CTX_PARTS)
CH = tuple(name for name, _ in CH_PARTS)
CTX_COUNT = 16
FILTER_ROWS = 96


def passed_along(value, axis, count, steps):
    initial, last = (max(0, -steps), min(count, count - steps))
    return lax.ppermute(value, axis, [(source, source + steps) for source in range(initial, last)])


def gathered(block, name, count):
    copies = jnp.broadcast_to(block[None], (count,) + block.shape)
    return lax.all_to_all(copies, name, 0, 0)


def reduced(stack, name, count):
    parts = lax.all_to_all(stack, name, 0, 0)
    total = parts[0].astype(jnp.float32)
    for member in range(1, count):
        total = total + parts[member].astype(jnp.float32)
    return total


def featurize(extended, feat_taps, count):
    feat_len = feat_taps.shape[1]
    chans = feat_taps.shape[2]
    shaped = extended.reshape(extended.shape[0], 3, chans)
    feats = jnp.zeros((count, 3, chans), jnp.float32)
    for tap in range(feat_len):
        feats = feats + feat_taps[:, tap, :] * shaped[
            feat_len - 1 - tap : feat_len - 1 - tap + count
        ].astype(jnp.float32)
    return feats


def filter_kernel(ext_ref, filt_ref, out_ref, shift_ref):
    taps = filt_ref.shape[0]
    rows = shift_ref.shape[1]
    count = out_ref.shape[0]
    for b in range(8):
        shift_ref[b] = ext_ref[pl.ds(8 - b, rows), :]

    def tile(index, carry):
        base = pl.multiple_of(index * FILTER_ROWS, 8)
        acc = jnp.zeros((FILTER_ROWS, out_ref.shape[1]), jnp.float32)
        for group in range(taps // 8):
            for b in range(8):
                tap = 8 * group + b
                acc = acc + filt_ref[pl.ds(tap, 1), :] * shift_ref[
                    b, pl.ds(base + taps - 8 - 8 * group, FILTER_ROWS), :
                ]
        out_ref[pl.ds(base, FILTER_ROWS), :] = acc
        return carry

    lax.fori_loop(0, count // FILTER_ROWS, tile, 0)


def causal_filter(extended, filt_rows):
    taps, chans = filt_rows.shape
    count = extended.shape[0] - taps
    rows = extended.shape[0] - 8
    return pl.pallas_call(
        filter_kernel,
        out_shape=jax.ShapeDtypeStruct((count, chans), jnp.float32),
        scratch_shapes=[pltpu.VMEM((8, rows, chans), jnp.float32)],
    )(extended, filt_rows)


def shards(bases_in, norm_gain, w_in, feat_taps, long_filter, skip_gain, w_out):
    tok, chans = bases_in.shape
    width = norm_gain.shape[0]
    taps = long_filter.shape[1]
    feat_len = feat_taps.shape[1]
    w_flat = w_in.reshape(width, 3 * chans)
    stacked = lax.all_gather(bases_in, CH[0], axis=0)
    for name, size in CH_PARTS[1:]:
        stacked = gathered(stacked, name, size)
    whole = stacked.transpose(3, 2, 1, 0, 4).reshape(tok, width)
    wide = whole.astype(jnp.float32)
    inverse = lax.rsqrt(jnp.mean(wide * wide, axis=1, keepdims=True) + 1e-05)
    normed = (wide * inverse * norm_gain).astype(jnp.bfloat16)
    mixed_in = jnp.dot(normed, w_flat, preferred_element_type=jnp.float32)
    projected = mixed_in.astype(jnp.bfloat16)
    earlier = passed_along(projected[tok - (taps - 1) - (feat_len - 1) :], CTX, CTX_COUNT, 1)
    local_feats = featurize(projected, feat_taps, tok - (feat_len - 1))
    local_product = (local_feats[:, 1, :] * local_feats[:, 2, :]).astype(jnp.bfloat16)
    filt_rows = long_filter.astype(jnp.float32).T
    half = tok // 2
    tail = causal_filter(local_product[half - taps - (feat_len - 1) :].astype(jnp.float32), filt_rows)
    tail, earlier = lax.optimization_barrier((tail, earlier))
    early_feats = featurize(earlier, feat_taps, taps - 1)
    before = (early_feats[:, 1, :] * early_feats[:, 2, :]).astype(jnp.bfloat16)
    head_feats = featurize(
        jnp.concatenate([earlier[earlier.shape[0] - (feat_len - 1) :], projected[: feat_len - 1]], axis=0),
        feat_taps,
        feat_len - 1,
    )
    query = jnp.concatenate([head_feats[:, 0, :], local_feats[:, 0, :]], axis=0)
    head_product = (head_feats[:, 1, :] * head_feats[:, 2, :]).astype(jnp.bfloat16)
    product = jnp.concatenate([head_product, local_product], axis=0)
    head = causal_filter(
        jnp.concatenate([jnp.zeros((1, chans), jnp.bfloat16), before, product[:half]], axis=0).astype(jnp.float32),
        filt_rows,
    )
    filtered = jnp.concatenate([head, tail], axis=0)
    gated = (query * (filtered + skip_gain * product.astype(jnp.float32))).astype(jnp.bfloat16)
    sizes = [size for _, size in CH_PARTS]
    blocks = w_out.reshape(chans, *sizes, chans).transpose(3, 2, 1, 0, 4)
    core = lax.axis_index(CH[2])
    mine = lax.dynamic_index_in_dim(blocks, core, 0, keepdims=False)
    theirs = lax.dynamic_index_in_dim(blocks, 1 - core, 0, keepdims=False)
    partner = lambda value: lax.ppermute(value, CH[2], [(0, 1), (1, 0)])
    own_part = jnp.einsum("tk,xzki->xzti", gated, mine, preferred_element_type=jnp.float32)
    their_part = jnp.einsum(
        "tk,xzki->xzti", partner(gated), partner(theirs), preferred_element_type=jnp.float32
    )
    split = (own_part + their_part).astype(jnp.bfloat16)
    for name, size in CH_PARTS[1::-1]:
        split = reduced(split, name, size).astype(jnp.bfloat16)
    return split


def solution(mesh):
    shape = [size for _, size in CTX_PARTS] + [size for _, size in CH_PARTS]
    fine = Mesh(mesh.devices.reshape(shape), CTX + CH)
    in_specs = (
        P(CTX, CH),
        P(),
        P(None, None, CH),
        P(None, None, CH),
        P(CH, None),
        P(CH),
        P(CH, None),
    )
    out_specs = P(CTX, CH)
    return jax.shard_map(shards, mesh=fine, in_specs=in_specs, out_specs=out_specs, check_vma=False)
```
